512 devices in a mesh: req: 32 (over x, y, core), ctx: 16 (over z).
Axes of the slice: x: 4, y: 4, z: 16, core: 2. Of those that a mesh axis runs over, the one named last changes fastest.
Arguments:
- queries: bfloat16 [64, 48, 8192], P('req', None, 'ctx'), parts along dimension 0, may hold values from -120 to 120
- key_cache: bfloat16 [64, 2048, 1024], P('req', 'ctx'), parts along dimension 0, may hold values from -5 to 5
- value_cache: bfloat16 [64, 2048, 1024], P('req', 'ctx'), parts along dimension 0, may hold values from -6 to 6
- draft_keys: bfloat16 [64, 48, 1024], P('req', None, 'ctx'), parts along dimension 0, may hold values from -12 to 12
- draft_values: bfloat16 [64, 48, 1024], P('req', None, 'ctx'), parts along dimension 0, may hold values from -6 to 6
- ancestors: int32 [64, 24, 24], P('req'), parts along dimension 0, may hold values from 0 to 1, as said below
- context_length: int32 [32], P('req'), parts along dimension 0, may hold values from 1025 to 2048
Outputs:
- attention: float32 [64, 48, 8192], P('req', None, 'ctx'), parts along dimension 0
The draws below stay inside these ranges and needn't reach their ends.
There are 32 independent parts, one for each index of `req`. The reference program is written for one: setup_inputs(seed, part) draws one part's arguments, and reference() takes and returns one part's arrays. A program takes and returns all parts, laid end to end along the dimension named above; each array names one. Nothing has to cross between parts.
Inputs may be any that keep to these rules, and one draw needn't show every extreme that they name: ancestors[t, n, j] is 1 exactly where node j of tree t is node n itself or one of its ancestors; node 0 is the root of every tree and every other node's parent has a lower number.
All inputs are finite; a program needn't handle non-finite values.
Results may differ from the reference program's by a relative error of at most 0.005.
Values may be sent and summed in bfloat16 or wider, within the bound.
No kernel may reach another device: no remote copies, remote signals or barrier semaphores. Data moves between devices by JAX's collectives and lax.ppermute only.
A program may use at most 64 MiB of HBM per device.

```python
import math
import jax
import jax.numpy as jnp
from jax import lax

H = 64
KVH = 8
DH = 128
LAYERS = 2
NODES = 24
TREES = 2
CTX_DEV = 128
TQ = 48
CONTEXT = 2048
N_CTX = 16


def joint_draw(key):
    key_keys = jax.random.fold_in(key, 11)
    key_queries = jax.random.fold_in(key, 12)
    cached = jnp.clip(jax.random.normal(key_keys, (LAYERS, CONTEXT, KVH * DH), jnp.float32), -5.0, 5.0)
    asked = jnp.clip(2.5 * jax.random.normal(key_queries, (LAYERS, TQ, H * DH), jnp.float32), -12.5, 12.5)
    return (cached.astype(jnp.bfloat16), asked.astype(jnp.bfloat16))


def draw_key_cache(key, part):
    return joint_draw(key)[0]


def draw_queries(key, part):
    return joint_draw(key)[1]


def draw_ancestors(key, part):
    picks = jax.random.randint(jax.random.fold_in(key, 21), (TREES, NODES), 0, 1 << 20)
    node_ids = jnp.arange(NODES, dtype=jnp.int32)
    parents = jnp.where(node_ids[None, :] > 0, picks % jnp.maximum(node_ids, 1)[None, :], 0)
    start = jnp.broadcast_to(jnp.eye(NODES, dtype=jnp.int32), (TREES, NODES, NODES))
    tree_ids = jnp.arange(TREES, dtype=jnp.int32)

    def extend(node_index, table):
        parent_rows = table[tree_ids, parents[:, node_index]]
        own_row = jnp.maximum(parent_rows, (node_ids == node_index).astype(jnp.int32)[None, :])
        return table.at[:, node_index].set(own_row)
    return lax.fori_loop(1, NODES, extend, start)


def block_scale(rng, shape, shards, least, largest):
    loudness = 1.0
    for axis_at, parts in shards:
        heights = jax.random.uniform(jax.random.fold_in(jax.random.fold_in(rng, 6), axis_at), (parts,), jnp.float32, least / len(shards), largest / len(shards))
        loudness = loudness * jnp.repeat(jnp.exp(heights), shape[axis_at] // parts).reshape((-1,) + (1,) * (len(shape) - 1 - axis_at))
    return loudness


def bell_draw(stream_key, extent, spread, reach, shards=(), held_as=jnp.bfloat16):
    level = block_scale(stream_key, extent, shards, -0.22, 0.18) if shards else 1.0
    array = jax.random.normal(stream_key, extent, jnp.float32) * spread * level
    return jnp.minimum(jnp.maximum(array, -reach), reach).astype(held_as)


def setup_inputs(seed: int = 0, part: int = 0) -> dict:
    seeds = jax.random.split(jax.random.key(seed), 8)
    own_keys = jax.random.split(jax.random.fold_in(seeds[7], part), 8)
    return {
        "queries": draw_queries(jax.random.fold_in(jax.random.fold_in(seeds[7], part), 71), part),
        "key_cache": draw_key_cache(jax.random.fold_in(jax.random.fold_in(seeds[7], part), 71), part),
        "value_cache": bell_draw(own_keys[2], (LAYERS, CONTEXT, KVH * DH), 1.0, 6.0, ((1, 16),)),
        "draft_keys": bell_draw(own_keys[3], (LAYERS, TQ, KVH * DH), 2.5, 12.0, ((2, 16),)),
        "draft_values": bell_draw(own_keys[4], (LAYERS, TQ, KVH * DH), 1.0, 6.0, ((2, 16),)),
        "ancestors": draw_ancestors(jax.random.fold_in(jax.random.fold_in(seeds[7], part), 71), part),
        "context_length": jax.random.randint(own_keys[6], (1,), CONTEXT // 2 + 1, CONTEXT + 1).astype(jnp.int32),
    }


masked_score = -1e+30

def block_partial(query_heads, block_keys, block_values, draft_k, draft_v, cache_keep, draft_keep, score_scale):
    scores = jnp.einsum('qkjd,pkd->kqjp', query_heads.astype(jnp.float32), block_keys.astype(jnp.float32)) * score_scale
    draft_scores = jnp.einsum('qkjd,tkd->kqjt', query_heads.astype(jnp.float32), draft_k.astype(jnp.float32)) * score_scale
    scores = jnp.where(cache_keep[None, None, None, :], scores, masked_score)
    draft_scores = jnp.where(draft_keep[None, :, None, :], draft_scores, masked_score)
    top_score = jnp.maximum(lax.optimization_barrier(jnp.max(scores, -1)), lax.optimization_barrier(jnp.max(draft_scores, -1)))
    cache_weight = jnp.where(cache_keep[None, None, None, :], jnp.exp(scores - top_score[..., None]), 0.0)
    draft_weight = jnp.where(draft_keep[None, :, None, :], jnp.exp(draft_scores - top_score[..., None]), 0.0)
    total = lax.optimization_barrier(jnp.sum(cache_weight, -1)) + lax.optimization_barrier(jnp.sum(draft_weight, -1))
    cache_rounded = cache_weight.astype(jnp.bfloat16).astype(jnp.float32)
    draft_rounded = draft_weight.astype(jnp.bfloat16).astype(jnp.float32)
    weighted = jnp.einsum('kqjp,pkd->qkjd', cache_rounded, block_values.astype(jnp.float32))
    weighted = weighted + jnp.einsum('kqjt,tkd->qkjd', draft_rounded, draft_v.astype(jnp.float32))
    top_score = jnp.transpose(top_score, (1, 0, 2))
    total = jnp.transpose(total, (1, 0, 2))
    alive = total > 0.0
    safe_total = jnp.where(alive, total, 1.0)
    output = jnp.where(alive[..., None], weighted / safe_total[..., None], 0.0).astype(jnp.bfloat16)
    lse = jnp.where(alive, top_score + jnp.log(safe_total), masked_score)
    return (lse, output)

def reference(queries, key_cache, value_cache, draft_keys, draft_values, ancestors, context_length):
    group_size = H // KVH
    score_scale = 1.0 / math.sqrt(DH)
    tree_keep = (jnp.eye(TREES, dtype=jnp.int32)[:, None, :, None] * ancestors[:, :, None, :]).reshape(TQ, TQ) > 0
    positions = jnp.arange(CTX_DEV, dtype=jnp.int32)
    results = []
    for layer_index in range(LAYERS):
        query_heads = queries[layer_index].reshape(TQ, KVH, group_size, DH)
        key_blocks = key_cache[layer_index].reshape(N_CTX, CTX_DEV, KVH, DH)
        value_blocks = value_cache[layer_index].reshape(N_CTX, CTX_DEV, KVH, DH)
        draft_k = draft_keys[layer_index].reshape(TQ, KVH, DH)
        draft_v = draft_values[layer_index].reshape(TQ, KVH, DH)

        def one_block(packed):
            block_index, block_keys, block_values = packed
            cache_keep = block_index * CTX_DEV + positions < context_length[0]
            draft_keep = jnp.logical_and(tree_keep, block_index == 0)
            return block_partial(query_heads, block_keys, block_values, draft_k, draft_v, cache_keep, draft_keep, score_scale)
        lses, outputs = lax.map(one_block, (jnp.arange(N_CTX, dtype=jnp.int32), key_blocks, value_blocks))
        outputs = lax.optimization_barrier(outputs).astype(jnp.float32)
        overall = lax.optimization_barrier(jnp.max(lses, 0))
        factor = jnp.exp(lses - overall)
        total = lax.optimization_barrier(jnp.sum(factor, 0))
        weighted = lax.optimization_barrier(jnp.sum(factor[..., None] * outputs, 0))
        results.append((weighted / total[..., None]).reshape(TQ, H * DH))
    return jnp.stack(results)
```

```python
import math

import jax
import jax.numpy as jnp
from jax import lax
from jax.sharding import PartitionSpec as P

H = 64
KVH = 8
DH = 128


masked_score = -1e30


def block_partial(query_heads, block_keys, block_values, draft_k, draft_v, cache_keep, draft_keep, score_scale):
    scores = (
        jnp.einsum("kaqid,pkd->kaqip", query_heads, block_keys, preferred_element_type=jnp.float32)
        * score_scale
    )
    draft_scores = (
        jnp.einsum("kaqid,tkd->kaqit", query_heads, draft_k, preferred_element_type=jnp.float32)
        * score_scale
    )
    scores = jnp.where(cache_keep[None, None, None, None, :], scores, masked_score)
    draft_scores = jnp.where(draft_keep[None, None, :, None, :], draft_scores, masked_score)
    top_score = jnp.maximum(jnp.max(scores, -1), jnp.max(draft_scores, -1))
    shift_by = jnp.where(top_score > -1e29, top_score, 0.0)
    cache_weight = jnp.exp(scores - shift_by[..., None])
    draft_weight = jnp.exp(draft_scores - shift_by[..., None])
    total = jnp.sum(cache_weight, -1) + jnp.sum(draft_weight, -1)
    weighted = jnp.einsum(
        "kaqip,pkd->kaiqd",
        cache_weight.astype(jnp.bfloat16),
        block_values,
        preferred_element_type=jnp.float32,
    )
    weighted = weighted + jnp.einsum(
        "kaqit,tkd->kaiqd",
        draft_weight.astype(jnp.bfloat16),
        draft_v,
        preferred_element_type=jnp.float32,
    )
    top_score = jnp.transpose(top_score, (0, 1, 3, 2))
    total = jnp.transpose(total, (0, 1, 3, 2))
    alive = total > 0.0
    safe_total = jnp.where(alive, total, 1.0)
    output = jnp.where(alive[..., None], weighted / safe_total[..., None], 0.0).astype(jnp.bfloat16)
    lse = jnp.where(alive, top_score + jnp.log(safe_total), masked_score)
    return (lse, output)


def body(queries, key_cache, value_cache, draft_keys, draft_values, ancestors, context_length):
    devices = lax.axis_size("ctx")
    device_index = lax.axis_index("ctx")
    layers, rows, q_cols = queries.shape
    kv_cols = draft_keys.shape[2]
    packed = jnp.concatenate([queries, draft_keys, draft_values], axis=2)
    gathered = lax.all_gather(packed, "ctx", axis=0)
    local_len = key_cache.shape[1]
    trees = ancestors.shape[0]
    group_size = H // KVH
    split = devices // KVH
    heads_here = H // devices
    score_scale = 1.0 / math.sqrt(DH)
    tree_keep = (
        jnp.eye(trees, dtype=jnp.int32)[:, None, :, None] * ancestors[:, :, None, :]
    ).reshape(rows, rows) > 0
    draft_keep = jnp.logical_and(tree_keep, device_index == 0)
    cache_keep = (
        device_index * local_len + jnp.arange(local_len, dtype=jnp.int32) < context_length[0]
    )
    results = []
    for layer_index in range(layers):
        g = gathered[:, layer_index]
        query_heads = g[:, :, :q_cols].reshape(KVH, split, rows, heads_here, DH)
        draft_k = g[:, :, q_cols:q_cols + kv_cols].reshape(KVH, split, rows, kv_cols)
        draft_k = jnp.transpose(draft_k, (2, 0, 1, 3)).reshape(rows, KVH, DH)
        draft_v = g[:, :, q_cols + kv_cols:].reshape(KVH, split, rows, kv_cols)
        draft_v = jnp.transpose(draft_v, (2, 0, 1, 3)).reshape(rows, KVH, DH)
        lse, output = block_partial(
            query_heads,
            key_cache[layer_index].reshape(local_len, KVH, DH),
            value_cache[layer_index].reshape(local_len, KVH, DH),
            draft_k,
            draft_v,
            cache_keep,
            draft_keep,
            score_scale,
        )
        lse = lse.reshape(devices, heads_here, rows)
        output = output.reshape(devices, heads_here, rows, DH).astype(jnp.float32)
        overall = lax.pmax(lse, "ctx")
        factor = jnp.exp(lse - overall)
        weighted = factor[..., None] * output
        weighted_mine = lax.psum_scatter(weighted, "ctx", scatter_dimension=0, tiled=True)[0]
        total_mine = lax.psum_scatter(factor, "ctx", scatter_dimension=0, tiled=True)[0]
        mine = weighted_mine / total_mine[..., None]
        results.append(jnp.transpose(mine, (1, 0, 2)).reshape(rows, heads_here * DH))
    return jnp.stack(results)


def solution(mesh):
    placed = (
        P("req", None, "ctx"),
        P("req", "ctx", None),
        P("req", "ctx", None),
        P("req", None, "ctx"),
        P("req", None, "ctx"),
        P("req", None, None),
        P("req"),
    )
    return jax.shard_map(
        body, mesh=mesh, in_specs=placed, out_specs=P("req", None, "ctx"), check_vma=False
    )
```

```python
import math

import jax
import jax.numpy as jnp
from jax import lax
from jax.sharding import PartitionSpec as P

H = 64
KVH = 8
DH = 128


masked_score = -1e30


def send_target(s, j, n):
    return (s + j) % n if (s + j) % 2 == 0 else (s - j) % n


def blocks_partial(query_heads, block_keys, block_values, draft_k, draft_v, cache_keep, draft_keep, score_scale):
    scores = (
        jnp.einsum("qhd,jpd->hqjp", query_heads, block_keys, preferred_element_type=jnp.float32)
        * score_scale
    )
    draft_scores = (
        jnp.einsum("qhd,td->hqt", query_heads, draft_k, preferred_element_type=jnp.float32)
        * score_scale
    )
    scores = jnp.where(cache_keep[None, None], scores, masked_score)
    draft_scores = jnp.where(draft_keep[None], draft_scores[:, :, None, :], masked_score)
    top_score = jnp.maximum(jnp.max(scores, -1), jnp.max(draft_scores, -1))
    shift_by = jnp.where(top_score > -1e29, top_score, 0.0)
    cache_weight = jnp.exp(scores - shift_by[..., None])
    draft_weight = jnp.exp(draft_scores - shift_by[..., None])
    total = jnp.sum(cache_weight, -1) + jnp.sum(draft_weight, -1)
    weighted = jnp.einsum(
        "hqjp,jpd->hqjd",
        cache_weight.astype(jnp.bfloat16),
        block_values,
        preferred_element_type=jnp.float32,
    )
    weighted = weighted + jnp.einsum(
        "hqjt,td->hqjd",
        draft_weight.astype(jnp.bfloat16),
        draft_v,
        preferred_element_type=jnp.float32,
    )
    alive = total > 0.0
    safe_total = jnp.where(alive, total, 1.0)
    output = lax.reduce_precision(
        jnp.where(alive[..., None], weighted / safe_total[..., None], 0.0), exponent_bits=8, mantissa_bits=7
    )
    lse = jnp.where(alive, top_score + jnp.log(safe_total), masked_score)
    top = jnp.max(lse, -1)
    factor = jnp.where(lse > -1e29, jnp.exp(lse - top[..., None]), 0.0)
    return top, jnp.sum(factor, -1), jnp.sum(factor[..., None] * output, 2)


def body(queries, key_cache, value_cache, draft_keys, draft_values, ancestors, context_length):
    n = lax.axis_size("ctx")
    d = lax.axis_index("ctx")
    assert n == 2 * KVH
    layers, rows, q_cols = queries.shape
    kv_cols = draft_keys.shape[2]
    local_len = key_cache.shape[1]
    trees = ancestors.shape[0]
    heads_here = H // n
    reach = n // 2
    score_scale = 1.0 / math.sqrt(DH)
    own = d % 2
    pair = d // 2
    swap = [(s, s ^ 1) for s in range(n)]

    packed = jnp.concatenate([queries, draft_keys, draft_values], axis=2)
    partner = lax.ppermute(packed, "ctx", swap)
    first = jnp.where(own == 0, packed, partner)
    second = jnp.where(own == 0, partner, packed)

    kv = jnp.stack(
        [key_cache.reshape(layers, local_len, KVH, DH), value_cache.reshape(layers, local_len, KVH, DH)], 1
    )
    kv = jnp.transpose(kv, (0, 3, 1, 2, 4))

    sources = jnp.where(own == 0, d - jnp.arange(reach), d + jnp.arange(reach)) % n
    tree_keep = (
        jnp.eye(trees, dtype=jnp.int32)[:, None, :, None] * ancestors[:, :, None, :]
    ).reshape(rows, rows) > 0
    cache_keep = sources[:, None] * local_len + jnp.arange(local_len)[None, :] < context_length[0]
    draft_keep = jnp.logical_and(tree_keep[:, None, :], (sources == 0)[None, :, None])

    results = []
    for layer_index in range(layers):
        here = kv[layer_index]
        blocks = [lax.dynamic_index_in_dim(here, pair, 0, keepdims=False)]
        for j in range(1, reach):
            target = jnp.where((d + j) % 2 == 0, (d + j) % n, (d - j) % n)
            msg = lax.dynamic_index_in_dim(here, target // 2, 0, keepdims=False)
            blocks.append(lax.ppermute(msg, "ctx", [(s, send_target(s, j, n)) for s in range(n)]))
        blocks = jnp.stack(blocks)
        f = first[layer_index]
        s2 = second[layer_index]
        query_heads = jnp.concatenate(
            [f[:, :q_cols].reshape(rows, heads_here, DH), s2[:, :q_cols].reshape(rows, heads_here, DH)], 1
        )
        draft_k = jnp.concatenate([f[:, q_cols:q_cols + kv_cols], s2[:, q_cols:q_cols + kv_cols]], 1)
        draft_v = jnp.concatenate([f[:, q_cols + kv_cols:], s2[:, q_cols + kv_cols:]], 1)
        top, total, acc = blocks_partial(
            query_heads, blocks[:, 0], blocks[:, 1], draft_k, draft_v, cache_keep, draft_keep, score_scale
        )
        top = top.reshape(2, heads_here, rows)
        total = total.reshape(2, heads_here, rows)
        acc = acc.reshape(2, heads_here, rows, DH)
        keep = (jnp.where(own == 0, top[0], top[1]), jnp.where(own == 0, total[0], total[1]),
                jnp.where(own == 0, acc[0], acc[1]))
        give = (jnp.where(own == 0, top[1], top[0]), jnp.where(own == 0, total[1], total[0]),
                jnp.where(own == 0, acc[1], acc[0]))
        got = lax.ppermute(give, "ctx", swap)
        overall = jnp.maximum(keep[0], got[0])
        f_keep = jnp.exp(keep[0] - overall)
        f_got = jnp.exp(got[0] - overall)
        mine = (keep[2] * f_keep[..., None] + got[2] * f_got[..., None]) / (
            keep[1] * f_keep + got[1] * f_got
        )[..., None]
        results.append(jnp.transpose(mine, (1, 0, 2)).reshape(rows, heads_here * DH))
    return jnp.stack(results)


def solution(mesh):
    placed = (
        P("req", None, "ctx"),
        P("req", "ctx", None),
        P("req", "ctx", None),
        P("req", None, "ctx"),
        P("req", None, "ctx"),
        P("req", None, None),
        P("req"),
    )
    return jax.shard_map(
        body, mesh=mesh, in_specs=placed, out_specs=P("req", None, "ctx"), check_vma=False
    )
```

```python
import math

import jax
import jax.numpy as jnp
from jax import lax
from jax.sharding import PartitionSpec as P

H = 64
KVH = 8
DH = 128


masked_score = -1e30


def send_target(s, j, n):
    return (s + j) % n if (s + j) % 2 == 0 else (s - j) % n


def blocks_partial(query_heads, block_keys, block_values, draft_k, draft_v, cache_keep, draft_keep, score_scale):
    scores = (
        jnp.einsum("qhd,jpd->hqjp", query_heads, block_keys, preferred_element_type=jnp.float32)
        * score_scale
    )
    draft_scores = (
        jnp.einsum("qhd,td->hqt", query_heads, draft_k, preferred_element_type=jnp.float32)
        * score_scale
    )
    scores = jnp.where(cache_keep[None, None], scores, masked_score)
    draft_scores = jnp.where(draft_keep[None], draft_scores[:, :, None, :], masked_score)
    top_score = jnp.maximum(jnp.max(scores, -1), jnp.max(draft_scores, -1))
    shift_by = jnp.where(top_score > -1e29, top_score, 0.0)
    cache_weight = jnp.exp(scores - shift_by[..., None])
    draft_weight = jnp.exp(draft_scores - shift_by[..., None])
    total = jnp.sum(cache_weight, -1) + jnp.sum(draft_weight, -1)
    weighted = jnp.einsum(
        "hqjp,jpd->hqjd",
        cache_weight.astype(jnp.bfloat16),
        block_values,
        preferred_element_type=jnp.float32,
    )
    weighted = weighted + jnp.einsum(
        "hqjt,td->hqjd",
        draft_weight.astype(jnp.bfloat16),
        draft_v,
        preferred_element_type=jnp.float32,
    )
    alive = total > 0.0
    safe_total = jnp.where(alive, total, 1.0)
    output = lax.reduce_precision(
        jnp.where(alive[..., None], weighted / safe_total[..., None], 0.0), exponent_bits=8, mantissa_bits=7
    )
    lse = jnp.where(alive, top_score + jnp.log(safe_total), masked_score)
    top = jnp.max(lse, -1)
    factor = jnp.where(lse > -1e29, jnp.exp(lse - top[..., None]), 0.0)
    return top, jnp.sum(factor, -1), jnp.sum(factor[..., None] * output, 2)


def body(queries, key_cache, value_cache, draft_keys, draft_values, ancestors, context_length):
    n = lax.axis_size("ctx")
    d = lax.axis_index("ctx")
    assert n == 2 * KVH
    layers, rows, q_cols = queries.shape
    kv_cols = draft_keys.shape[2]
    local_len = key_cache.shape[1]
    trees = ancestors.shape[0]
    heads_here = H // n
    reach = n // 2
    score_scale = 1.0 / math.sqrt(DH)
    own = d % 2
    pair = d // 2
    swap = [(s, s ^ 1) for s in range(n)]

    packed = jnp.concatenate([queries, draft_keys, draft_values], axis=2)
    partner = lax.ppermute(packed, "ctx", swap)
    first = jnp.where(own == 0, packed, partner)
    second = jnp.where(own == 0, partner, packed)

    kv = jnp.stack(
        [key_cache.reshape(layers, local_len, KVH, DH), value_cache.reshape(layers, local_len, KVH, DH)], 1
    )
    kv = jnp.transpose(kv, (3, 0, 1, 2, 4))

    sources = jnp.where(own == 0, d - jnp.arange(reach), d + jnp.arange(reach)) % n
    tree_keep = (
        jnp.eye(trees, dtype=jnp.int32)[:, None, :, None] * ancestors[:, :, None, :]
    ).reshape(rows, rows) > 0
    cache_keep = sources[:, None] * local_len + jnp.arange(local_len)[None, :] < context_length[0]
    draft_keep = jnp.logical_and(tree_keep[:, None, :], (sources == 0)[None, :, None])

    blocks = [lax.dynamic_index_in_dim(kv, pair, 0, keepdims=False)]
    for j in range(1, reach):
        target = jnp.where((d + j) % 2 == 0, (d + j) % n, (d - j) % n)
        msg = lax.dynamic_index_in_dim(kv, target // 2, 0, keepdims=False)
        blocks.append(lax.ppermute(msg, "ctx", [(s, send_target(s, j, n)) for s in range(n)]))
    blocks = jnp.stack(blocks, 1)

    keeps, gives = [], []
    for layer_index in range(layers):
        f = first[layer_index]
        s2 = second[layer_index]
        query_heads = jnp.concatenate(
            [f[:, :q_cols].reshape(rows, heads_here, DH), s2[:, :q_cols].reshape(rows, heads_here, DH)], 1
        )
        draft_k = jnp.concatenate([f[:, q_cols:q_cols + kv_cols], s2[:, q_cols:q_cols + kv_cols]], 1)
        draft_v = jnp.concatenate([f[:, q_cols + kv_cols:], s2[:, q_cols + kv_cols:]], 1)
        here = blocks[layer_index]
        top, total, acc = blocks_partial(
            query_heads, here[:, 0], here[:, 1], draft_k, draft_v, cache_keep, draft_keep, score_scale
        )
        stats = jnp.concatenate([top, total, jnp.zeros((top.shape[0], DH - 2 * rows), jnp.float32)], 1)
        merged = jnp.concatenate([acc, stats[:, None, :]], 1).reshape(2, heads_here, rows + 1, DH)
        keeps.append(jnp.where(own == 0, merged[0], merged[1]))
        gives.append(jnp.where(own == 0, merged[1], merged[0]))
    keeps = jnp.stack(keeps)
    gots = lax.ppermute(jnp.stack(gives), "ctx", swap)
    results = []
    for layer_index in range(layers):
        keep, got = keeps[layer_index], gots[layer_index]
        top_keep, total_keep = keep[:, rows, :rows], keep[:, rows, rows:2 * rows]
        top_got, total_got = got[:, rows, :rows], got[:, rows, rows:2 * rows]
        overall = jnp.maximum(top_keep, top_got)
        f_keep = jnp.exp(top_keep - overall)
        f_got = jnp.exp(top_got - overall)
        mine = (keep[:, :rows] * f_keep[..., None] + got[:, :rows] * f_got[..., None]) / (
            total_keep * f_keep + total_got * f_got
        )[..., None]
        results.append(jnp.transpose(mine, (1, 0, 2)).reshape(rows, heads_here * DH))
    return jnp.stack(results)


def solution(mesh):
    placed = (
        P("req", None, "ctx"),
        P("req", "ctx", None),
        P("req", "ctx", None),
        P("req", None, "ctx"),
        P("req", None, "ctx"),
        P("req", None, None),
        P("req"),
    )
    return jax.shard_map(
        body, mesh=mesh, in_specs=placed, out_specs=P("req", None, "ctx"), check_vma=False
    )
```

```python
import math

import jax
import jax.numpy as jnp
from jax import lax
from jax.sharding import PartitionSpec as P

H = 64
KVH = 8
DH = 128


masked_score = -1e30


def send_target(s, j, n):
    return (s + j) % n if (s + j) % 2 == 0 else (s - j) % n


def blocks_partial(query_heads, block_keys, block_values, draft_k, draft_v, cache_keep, draft_keep, score_scale):
    scores = (
        jnp.einsum("qhd,jpd->hqjp", query_heads, block_keys, preferred_element_type=jnp.float32)
        * score_scale
    )
    draft_scores = (
        jnp.einsum("qhd,td->hqt", query_heads, draft_k, preferred_element_type=jnp.float32)
        * score_scale
    )
    scores = jnp.where(cache_keep[None, None], scores, masked_score)
    draft_scores = jnp.where(draft_keep[None], draft_scores[:, :, None, :], masked_score)
    top_score = jnp.maximum(jnp.max(scores, -1), jnp.max(draft_scores, -1))
    shift_by = jnp.where(top_score > -1e29, top_score, 0.0)
    cache_weight = jnp.exp(scores - shift_by[..., None])
    draft_weight = jnp.exp(draft_scores - shift_by[..., None])
    total = jnp.sum(cache_weight, -1) + jnp.sum(draft_weight, -1)
    weighted = jnp.einsum(
        "hqjp,jpd->hqjd",
        cache_weight.astype(jnp.bfloat16),
        block_values,
        preferred_element_type=jnp.float32,
    )
    weighted = weighted + jnp.einsum(
        "hqjt,td->hqjd",
        draft_weight.astype(jnp.bfloat16),
        draft_v,
        preferred_element_type=jnp.float32,
    )
    alive = total > 0.0
    safe_total = jnp.where(alive, total, 1.0)
    output = lax.reduce_precision(
        jnp.where(alive[..., None], weighted / safe_total[..., None], 0.0), exponent_bits=8, mantissa_bits=7
    )
    lse = jnp.where(alive, top_score + jnp.log(safe_total), masked_score)
    top = jnp.max(lse, -1)
    factor = jnp.where(lse > -1e29, jnp.exp(lse - top[..., None]), 0.0)
    return top, jnp.sum(factor, -1), jnp.sum(factor[..., None] * output, 2)


def body(queries, key_cache, value_cache, draft_keys, draft_values, ancestors, context_length):
    n = lax.axis_size("ctx")
    d = lax.axis_index("ctx")
    layers, rows, q_cols = queries.shape
    assert n == KVH * layers
    kv_cols = draft_keys.shape[2]
    local_len = key_cache.shape[1]
    trees = ancestors.shape[0]
    heads_here = H // n
    score_scale = 1.0 / math.sqrt(DH)
    own = d % layers
    swap = [(s, s ^ 1) for s in range(n)]

    packed = jnp.concatenate([queries, draft_keys, draft_values], axis=2)
    mine_now = lax.dynamic_index_in_dim(packed, own, 0, keepdims=False)
    partner = lax.ppermute(lax.dynamic_index_in_dim(packed, 1 - own, 0, keepdims=False), "ctx", swap)
    first = jnp.where(own == 0, mine_now, partner)
    second = jnp.where(own == 0, partner, mine_now)

    kv = jnp.stack(
        [key_cache.reshape(layers, local_len, KVH, DH), value_cache.reshape(layers, local_len, KVH, DH)], 1
    )
    kv = jnp.transpose(kv, (3, 0, 1, 2, 4)).reshape(n, 2, local_len, DH)
    blocks = lax.all_to_all(kv, "ctx", 0, 0, tiled=True)

    sources = jnp.arange(n)
    tree_keep = (
        jnp.eye(trees, dtype=jnp.int32)[:, None, :, None] * ancestors[:, :, None, :]
    ).reshape(rows, rows) > 0
    cache_keep = sources[:, None] * local_len + jnp.arange(local_len)[None, :] < context_length[0]
    draft_keep = jnp.logical_and(tree_keep[:, None, :], (sources == 0)[None, :, None])

    query_heads = jnp.concatenate(
        [first[:, :q_cols].reshape(rows, heads_here, DH), second[:, :q_cols].reshape(rows, heads_here, DH)], 1
    )
    draft_k = jnp.concatenate([first[:, q_cols:q_cols + kv_cols], second[:, q_cols:q_cols + kv_cols]], 1)
    draft_v = jnp.concatenate([first[:, q_cols + kv_cols:], second[:, q_cols + kv_cols:]], 1)
    top, total, acc = blocks_partial(
        query_heads, blocks[:, 0], blocks[:, 1], draft_k, draft_v, cache_keep, draft_keep, score_scale
    )
    done = (acc / total[..., None]).reshape(2, heads_here, rows, DH)
    keep = jnp.where(own == 0, done[0], done[1])
    got = lax.ppermute(jnp.where(own == 0, done[1], done[0]), "ctx", swap)
    keep = jnp.transpose(keep, (1, 0, 2)).reshape(rows, heads_here * DH)
    got = jnp.transpose(got, (1, 0, 2)).reshape(rows, heads_here * DH)
    return jnp.stack([jnp.where(own == 0, keep, got), jnp.where(own == 0, got, keep)])


def solution(mesh):
    placed = (
        P("req", None, "ctx"),
        P("req", "ctx", None),
        P("req", "ctx", None),
        P("req", None, "ctx"),
        P("req", None, "ctx"),
        P("req", None, None),
        P("req"),
    )
    return jax.shard_map(
        body, mesh=mesh, in_specs=placed, out_specs=P("req", None, "ctx"), check_vma=False
    )
```

```python
import math

import jax
import jax.numpy as jnp
from jax import lax
from jax.experimental import pallas as pl
from jax.experimental.pallas import tpu as pltpu
from jax.sharding import PartitionSpec as P

H = 64
KVH = 8
DH = 128


masked_score = -1e30


def send_target(s, j, n):
    return (s + j) % n if (s + j) % 2 == 0 else (s - j) % n


def blocks_partial(query_heads, block_keys, block_values, draft_k, draft_v, cache_keep, draft_keep, score_scale):
    scores = (
        jnp.einsum("qhd,jpd->hqjp", query_heads, block_keys, preferred_element_type=jnp.float32)
        * score_scale
    )
    draft_scores = (
        jnp.einsum("qhd,td->hqt", query_heads, draft_k, preferred_element_type=jnp.float32)
        * score_scale
    )
    scores = jnp.where(cache_keep[None, None], scores, masked_score)
    draft_scores = jnp.where(draft_keep[None], draft_scores[:, :, None, :], masked_score)
    top_score = jnp.maximum(jnp.max(scores, -1), jnp.max(draft_scores, -1))
    shift_by = jnp.where(top_score > -1e29, top_score, 0.0)
    cache_weight = jnp.exp(scores - shift_by[..., None])
    draft_weight = jnp.exp(draft_scores - shift_by[..., None])
    total = jnp.sum(cache_weight, -1) + jnp.sum(draft_weight, -1)
    weighted = jnp.einsum(
        "hqjp,jpd->hqjd",
        cache_weight.astype(jnp.bfloat16),
        block_values,
        preferred_element_type=jnp.float32,
    )
    weighted = weighted + jnp.einsum(
        "hqjt,td->hqjd",
        draft_weight.astype(jnp.bfloat16),
        draft_v,
        preferred_element_type=jnp.float32,
    )
    alive = total > 0.0
    safe_total = jnp.where(alive, total, 1.0)
    output = lax.reduce_precision(
        jnp.where(alive[..., None], weighted / safe_total[..., None], 0.0), exponent_bits=8, mantissa_bits=7
    )
    lse = jnp.where(alive, top_score + jnp.log(safe_total), masked_score)
    top = jnp.max(lse, -1)
    factor = jnp.where(lse > -1e29, jnp.exp(lse - top[..., None]), 0.0)
    return top, jnp.sum(factor, -1), jnp.sum(factor[..., None] * output, 2)


def _dot(a, b, dims):
    return lax.dot_general(a, b, dims, preferred_element_type=jnp.float32)


def attend_kernel(len_ref, q_ref, k_ref, v_ref, dk_ref, dv_ref, tree_ref, o_ref, out_sc, lse_sc):
    blocks, block_len, _ = k_ref.shape
    score_scale = 1.0 / math.sqrt(DH)
    nt = (((1,), (1,)), ((), ()))
    nn = (((1,), (0,)), ((), ()))
    q = q_ref[...]
    ctx_len = len_ref[0]
    for j in range(blocks):
        scores = _dot(q, k_ref[j], nt) * score_scale
        pos = j * block_len + lax.broadcasted_iota(jnp.int32, scores.shape, 1)
        scores = jnp.where(pos < ctx_len, scores, masked_score)
        top = jnp.max(scores, axis=1, keepdims=True)
        if j == 0:
            draft = _dot(q, dk_ref[...], nt) * score_scale
            draft = jnp.where(tree_ref[...] > 0, draft, masked_score)
            top = jnp.maximum(top, jnp.max(draft, axis=1, keepdims=True))
        shift = jnp.where(top > -1e29, top, 0.0)
        weight = jnp.exp(scores - shift)
        total = jnp.sum(weight, axis=1, keepdims=True)
        acc = _dot(weight.astype(jnp.bfloat16), v_ref[j], nn)
        if j == 0:
            draft_weight = jnp.exp(draft - shift)
            total = total + jnp.sum(draft_weight, axis=1, keepdims=True)
            acc = acc + _dot(draft_weight.astype(jnp.bfloat16), dv_ref[...], nn)
        alive = total > 0.0
        safe = jnp.where(alive, total, 1.0)
        out_sc[j] = jnp.where(alive, acc / safe, 0.0).astype(jnp.bfloat16).astype(jnp.float32)
        lse_sc[:, j:j + 1] = jnp.where(alive, top + jnp.log(safe), masked_score)
    lse = lse_sc[...]
    overall = jnp.max(lse, axis=1, keepdims=True)
    factor = jnp.exp(lse - overall)
    weighted = factor[:, 0:1] * out_sc[0]
    for j in range(1, blocks):
        weighted = weighted + factor[:, j:j + 1] * out_sc[j]
    o_ref[...] = weighted / jnp.sum(factor, axis=1, keepdims=True)


def attend(context_length, q_rows, block_keys, block_values, draft_k, draft_v, tree_rows):
    rows = q_rows.shape[0]
    blocks = block_keys.shape[0]
    vmem = pl.BlockSpec(memory_space=pltpu.VMEM)
    return pl.pallas_call(
        attend_kernel,
        out_shape=jax.ShapeDtypeStruct((rows, DH), jnp.float32),
        in_specs=[pl.BlockSpec(memory_space=pltpu.SMEM)] + [vmem] * 6,
        out_specs=vmem,
        scratch_shapes=[pltpu.VMEM((blocks, rows, DH), jnp.float32), pltpu.VMEM((rows, blocks), jnp.float32)],
    )(context_length, q_rows, block_keys, block_values, draft_k, draft_v, tree_rows)


def body(queries, key_cache, value_cache, draft_keys, draft_values, ancestors, context_length):
    n = lax.axis_size("ctx")
    d = lax.axis_index("ctx")
    layers, rows, q_cols = queries.shape
    assert n == KVH * layers
    kv_cols = draft_keys.shape[2]
    local_len = key_cache.shape[1]
    trees = ancestors.shape[0]
    heads_here = H // n
    score_scale = 1.0 / math.sqrt(DH)
    own = d % layers
    swap = [(s, s ^ 1) for s in range(n)]

    packed = jnp.concatenate([queries, draft_keys, draft_values], axis=2)
    mine_now = lax.dynamic_index_in_dim(packed, own, 0, keepdims=False)
    partner = lax.ppermute(lax.dynamic_index_in_dim(packed, 1 - own, 0, keepdims=False), "ctx", swap)
    first = jnp.where(own == 0, mine_now, partner)
    second = jnp.where(own == 0, partner, mine_now)

    kv = jnp.stack(
        [key_cache.reshape(layers, local_len, KVH, DH), value_cache.reshape(layers, local_len, KVH, DH)], 1
    )
    kv = jnp.transpose(kv, (3, 0, 1, 2, 4)).reshape(n, 2, local_len, DH)
    blocks = lax.all_to_all(kv, "ctx", 0, 0, tiled=True)

    tree_keep = (
        jnp.eye(trees, dtype=jnp.int32)[:, None, :, None] * ancestors[:, :, None, :]
    ).reshape(rows, rows)
    pair_heads = 2 * heads_here
    query_heads = jnp.concatenate(
        [first[:, :q_cols].reshape(rows, heads_here, DH), second[:, :q_cols].reshape(rows, heads_here, DH)], 1
    )
    q_rows = jnp.transpose(query_heads, (1, 0, 2)).reshape(pair_heads * rows, DH)
    draft_k = jnp.concatenate([first[:, q_cols:q_cols + kv_cols], second[:, q_cols:q_cols + kv_cols]], 1)
    draft_v = jnp.concatenate([first[:, q_cols + kv_cols:], second[:, q_cols + kv_cols:]], 1)
    tree_rows = jnp.tile(tree_keep, (pair_heads, 1))
    done = attend(context_length, q_rows, blocks[:, 0], blocks[:, 1], draft_k, draft_v, tree_rows)
    done = done.reshape(2, heads_here, rows, DH)
    keep = jnp.where(own == 0, done[0], done[1])
    got = lax.ppermute(jnp.where(own == 0, done[1], done[0]), "ctx", swap)
    keep = jnp.transpose(keep, (1, 0, 2)).reshape(rows, heads_here * DH)
    got = jnp.transpose(got, (1, 0, 2)).reshape(rows, heads_here * DH)
    return jnp.stack([jnp.where(own == 0, keep, got), jnp.where(own == 0, got, keep)])


def solution(mesh):
    placed = (
        P("req", None, "ctx"),
        P("req", "ctx", None),
        P("req", "ctx", None),
        P("req", None, "ctx"),
        P("req", None, "ctx"),
        P("req", None, None),
        P("req"),
    )
    return jax.shard_map(
        body, mesh=mesh, in_specs=placed, out_specs=P("req", None, "ctx"), check_vma=False
    )
```

```python
import math

import jax
import jax.numpy as jnp
from jax import lax
from jax.experimental import pallas as pl
from jax.experimental.pallas import tpu as pltpu
from jax.sharding import PartitionSpec as P

H = 64
KVH = 8
DH = 128


masked_score = -1e30


def send_target(s, j, n):
    return (s + j) % n if (s + j) % 2 == 0 else (s - j) % n


def blocks_partial(query_heads, block_keys, block_values, draft_k, draft_v, cache_keep, draft_keep, score_scale):
    scores = (
        jnp.einsum("qhd,jpd->hqjp", query_heads, block_keys, preferred_element_type=jnp.float32)
        * score_scale
    )
    draft_scores = (
        jnp.einsum("qhd,td->hqt", query_heads, draft_k, preferred_element_type=jnp.float32)
        * score_scale
    )
    scores = jnp.where(cache_keep[None, None], scores, masked_score)
    draft_scores = jnp.where(draft_keep[None], draft_scores[:, :, None, :], masked_score)
    top_score = jnp.maximum(jnp.max(scores, -1), jnp.max(draft_scores, -1))
    shift_by = jnp.where(top_score > -1e29, top_score, 0.0)
    cache_weight = jnp.exp(scores - shift_by[..., None])
    draft_weight = jnp.exp(draft_scores - shift_by[..., None])
    total = jnp.sum(cache_weight, -1) + jnp.sum(draft_weight, -1)
    weighted = jnp.einsum(
        "hqjp,jpd->hqjd",
        cache_weight.astype(jnp.bfloat16),
        block_values,
        preferred_element_type=jnp.float32,
    )
    weighted = weighted + jnp.einsum(
        "hqjt,td->hqjd",
        draft_weight.astype(jnp.bfloat16),
        draft_v,
        preferred_element_type=jnp.float32,
    )
    alive = total > 0.0
    safe_total = jnp.where(alive, total, 1.0)
    output = lax.reduce_precision(
        jnp.where(alive[..., None], weighted / safe_total[..., None], 0.0), exponent_bits=8, mantissa_bits=7
    )
    lse = jnp.where(alive, top_score + jnp.log(safe_total), masked_score)
    top = jnp.max(lse, -1)
    factor = jnp.where(lse > -1e29, jnp.exp(lse - top[..., None]), 0.0)
    return top, jnp.sum(factor, -1), jnp.sum(factor[..., None] * output, 2)


def _dot(a, b, dims):
    return lax.dot_general(a, b, dims, preferred_element_type=jnp.float32)


def attend_kernel(len_ref, q_ref, kv_ref, dk_ref, dv_ref, tree_ref, o_ref, out_sc, lse_sc):
    blocks, _, block_len, _ = kv_ref.shape
    score_scale = 1.0 / math.sqrt(DH)
    nt = (((1,), (1,)), ((), ()))
    nn = (((1,), (0,)), ((), ()))
    q = q_ref[...]
    ctx_len = len_ref[0]
    for j in range(blocks):
        scores = _dot(q, kv_ref[j, 0], nt) * score_scale
        pos = j * block_len + lax.broadcasted_iota(jnp.int32, scores.shape, 1)
        scores = jnp.where(pos < ctx_len, scores, masked_score)
        top = jnp.max(scores, axis=1, keepdims=True)
        if j == 0:
            draft = _dot(q, dk_ref[...], nt) * score_scale
            draft = jnp.where(tree_ref[...] > 0, draft, masked_score)
            top = jnp.maximum(top, jnp.max(draft, axis=1, keepdims=True))
        shift = jnp.where(top > -1e29, top, 0.0)
        weight = jnp.exp(scores - shift)
        total = jnp.sum(weight, axis=1, keepdims=True)
        acc = _dot(weight.astype(jnp.bfloat16), kv_ref[j, 1], nn)
        if j == 0:
            draft_weight = jnp.exp(draft - shift)
            total = total + jnp.sum(draft_weight, axis=1, keepdims=True)
            acc = acc + _dot(draft_weight.astype(jnp.bfloat16), dv_ref[...], nn)
        alive = total > 0.0
        safe = jnp.where(alive, total, 1.0)
        out_sc[j] = jnp.where(alive, acc / safe, 0.0).astype(jnp.bfloat16).astype(jnp.float32)
        lse_sc[:, j:j + 1] = jnp.where(alive, top + jnp.log(safe), masked_score)
    lse = lse_sc[...]
    overall = jnp.max(lse, axis=1, keepdims=True)
    factor = jnp.exp(lse - overall)
    weighted = factor[:, 0:1] * out_sc[0]
    for j in range(1, blocks):
        weighted = weighted + factor[:, j:j + 1] * out_sc[j]
    o_ref[...] = weighted / jnp.sum(factor, axis=1, keepdims=True)


def attend(context_length, q_rows, blocks_kv, draft_k, draft_v, tree_rows):
    rows = q_rows.shape[0]
    blocks = blocks_kv.shape[0]
    vmem = pl.BlockSpec(memory_space=pltpu.VMEM)
    return pl.pallas_call(
        attend_kernel,
        out_shape=jax.ShapeDtypeStruct((rows, DH), jnp.float32),
        in_specs=[pl.BlockSpec(memory_space=pltpu.SMEM)] + [vmem] * 5,
        out_specs=vmem,
        scratch_shapes=[pltpu.VMEM((blocks, rows, DH), jnp.float32), pltpu.VMEM((rows, blocks), jnp.float32)],
    )(context_length, q_rows, blocks_kv, draft_k, draft_v, tree_rows)


def body(queries, key_cache, value_cache, draft_keys, draft_values, ancestors, context_length):
    n = lax.axis_size("ctx")
    d = lax.axis_index("ctx")
    layers, rows, q_cols = queries.shape
    assert n == KVH * layers
    kv_cols = draft_keys.shape[2]
    local_len = key_cache.shape[1]
    trees = ancestors.shape[0]
    heads_here = H // n
    score_scale = 1.0 / math.sqrt(DH)
    own = d % layers
    swap = [(s, s ^ 1) for s in range(n)]

    packed = jnp.concatenate([queries, draft_keys, draft_values], axis=2)
    mine_now = lax.dynamic_index_in_dim(packed, own, 0, keepdims=False)
    partner = lax.ppermute(lax.dynamic_index_in_dim(packed, 1 - own, 0, keepdims=False), "ctx", swap)
    first = jnp.where(own == 0, mine_now, partner)
    second = jnp.where(own == 0, partner, mine_now)

    kv = jnp.stack(
        [key_cache.reshape(layers, local_len, KVH, DH), value_cache.reshape(layers, local_len, KVH, DH)], 1
    )
    kv = jnp.transpose(kv, (3, 0, 1, 2, 4)).reshape(n, 2, local_len, DH)
    blocks = lax.all_to_all(kv, "ctx", 0, 0, tiled=True)

    tree_keep = (
        jnp.eye(trees, dtype=jnp.int32)[:, None, :, None] * ancestors[:, :, None, :]
    ).reshape(rows, rows)
    own_q = mine_now[:, :q_cols].reshape(rows, heads_here, DH)
    other_q = partner[:, :q_cols].reshape(rows, heads_here, DH)
    draft_k = jnp.concatenate([first[:, q_cols:q_cols + kv_cols], second[:, q_cols:q_cols + kv_cols]], 1)
    draft_v = jnp.concatenate([first[:, q_cols + kv_cols:], second[:, q_cols + kv_cols:]], 1)
    tree_rows = jnp.tile(tree_keep, (heads_here, 1))
    give = attend(context_length, jnp.transpose(other_q, (1, 0, 2)).reshape(heads_here * rows, DH),
                  blocks, draft_k, draft_v, tree_rows)
    got = lax.ppermute(give.reshape(heads_here, rows, DH), "ctx", swap)
    keep = attend(context_length, jnp.transpose(own_q, (1, 0, 2)).reshape(heads_here * rows, DH),
                  blocks, draft_k, draft_v, tree_rows).reshape(heads_here, rows, DH)
    keep = jnp.transpose(keep, (1, 0, 2)).reshape(rows, heads_here * DH)
    got = jnp.transpose(got, (1, 0, 2)).reshape(rows, heads_here * DH)
    return jnp.stack([jnp.where(own == 0, keep, got), jnp.where(own == 0, got, keep)])


def solution(mesh):
    placed = (
        P("req", None, "ctx"),
        P("req", "ctx", None),
        P("req", "ctx", None),
        P("req", None, "ctx"),
        P("req", None, "ctx"),
        P("req", None, None),
        P("req"),
    )
    return jax.shard_map(
        body, mesh=mesh, in_specs=placed, out_specs=P("req", None, "ctx"), check_vma=False
    )
```

```python
import math

import jax
import jax.numpy as jnp
from jax import lax
from jax.experimental import pallas as pl
from jax.experimental.pallas import tpu as pltpu
from jax.sharding import PartitionSpec as P

H = 64
KVH = 8
DH = 128


masked_score = -1e30


def send_target(s, j, n):
    return (s + j) % n if (s + j) % 2 == 0 else (s - j) % n


def blocks_partial(query_heads, block_keys, block_values, draft_k, draft_v, cache_keep, draft_keep, score_scale):
    scores = (
        jnp.einsum("qhd,jpd->hqjp", query_heads, block_keys, preferred_element_type=jnp.float32)
        * score_scale
    )
    draft_scores = (
        jnp.einsum("qhd,td->hqt", query_heads, draft_k, preferred_element_type=jnp.float32)
        * score_scale
    )
    scores = jnp.where(cache_keep[None, None], scores, masked_score)
    draft_scores = jnp.where(draft_keep[None], draft_scores[:, :, None, :], masked_score)
    top_score = jnp.maximum(jnp.max(scores, -1), jnp.max(draft_scores, -1))
    shift_by = jnp.where(top_score > -1e29, top_score, 0.0)
    cache_weight = jnp.exp(scores - shift_by[..., None])
    draft_weight = jnp.exp(draft_scores - shift_by[..., None])
    total = jnp.sum(cache_weight, -1) + jnp.sum(draft_weight, -1)
    weighted = jnp.einsum(
        "hqjp,jpd->hqjd",
        cache_weight.astype(jnp.bfloat16),
        block_values,
        preferred_element_type=jnp.float32,
    )
    weighted = weighted + jnp.einsum(
        "hqjt,td->hqjd",
        draft_weight.astype(jnp.bfloat16),
        draft_v,
        preferred_element_type=jnp.float32,
    )
    alive = total > 0.0
    safe_total = jnp.where(alive, total, 1.0)
    output = lax.reduce_precision(
        jnp.where(alive[..., None], weighted / safe_total[..., None], 0.0), exponent_bits=8, mantissa_bits=7
    )
    lse = jnp.where(alive, top_score + jnp.log(safe_total), masked_score)
    top = jnp.max(lse, -1)
    factor = jnp.where(lse > -1e29, jnp.exp(lse - top[..., None]), 0.0)
    return top, jnp.sum(factor, -1), jnp.sum(factor[..., None] * output, 2)


def _dot(a, b, dims):
    return lax.dot_general(a, b, dims, preferred_element_type=jnp.float32)


def attend_kernel(len_ref, q_ref, kv_ref, dk_ref, dvt_ref, tree_ref, o_ref, out_sc, lse_sc):
    blocks, _, block_len, _ = kv_ref.shape
    score_scale = 1.0 / math.sqrt(DH)
    nt = (((1,), (1,)), ((), ()))
    nn = (((1,), (0,)), ((), ()))
    q = q_ref[...]
    ctx_len = len_ref[0]
    for j in range(blocks):
        scores = _dot(kv_ref[j, 0], q, nt) * score_scale
        pos = j * block_len + lax.broadcasted_iota(jnp.int32, scores.shape, 0)
        scores = jnp.where(pos < ctx_len, scores, masked_score)
        top = jnp.max(scores, axis=0, keepdims=True)
        if j == 0:
            draft = _dot(dk_ref[...], q, nt) * score_scale
            draft = jnp.where(tree_ref[...] > 0, draft, masked_score)
            top = jnp.maximum(top, jnp.max(draft, axis=0, keepdims=True))
        shift = jnp.where(top > -1e29, top, 0.0)
        weight = jnp.exp(scores - shift)
        total = jnp.sum(weight, axis=0, keepdims=True)
        acc = _dot(kv_ref[j, 1], weight.astype(jnp.bfloat16), nn)
        if j == 0:
            draft_weight = jnp.exp(draft - shift)
            total = total + jnp.sum(draft_weight, axis=0, keepdims=True)
            acc = acc + _dot(dvt_ref[...], draft_weight.astype(jnp.bfloat16), nn)
        alive = total > 0.0
        safe = jnp.where(alive, total, 1.0)
        out_sc[j] = jnp.where(alive, acc / safe, 0.0).astype(jnp.bfloat16).astype(jnp.float32)
        lse_sc[j:j + 1, :] = jnp.where(alive, top + jnp.log(safe), masked_score)
    lse = lse_sc[...]
    overall = jnp.max(lse, axis=0, keepdims=True)
    factor = jnp.exp(lse - overall)
    weighted = factor[0:1] * out_sc[0]
    for j in range(1, blocks):
        weighted = weighted + factor[j:j + 1] * out_sc[j]
    o_ref[...] = weighted / jnp.sum(factor, axis=0, keepdims=True)


def attend(context_length, q_rows, blocks_kv, draft_k, draft_vt, tree_cols):
    rows = q_rows.shape[0]
    blocks = blocks_kv.shape[0]
    vmem = pl.BlockSpec(memory_space=pltpu.VMEM)
    return pl.pallas_call(
        attend_kernel,
        out_shape=jax.ShapeDtypeStruct((DH, rows), jnp.float32),
        in_specs=[pl.BlockSpec(memory_space=pltpu.SMEM)] + [vmem] * 5,
        out_specs=vmem,
        scratch_shapes=[pltpu.VMEM((blocks, DH, rows), jnp.float32), pltpu.VMEM((blocks, rows), jnp.float32)],
    )(context_length, q_rows, blocks_kv, draft_k, draft_vt, tree_cols)


def body(queries, key_cache, value_cache, draft_keys, draft_values, ancestors, context_length):
    n = lax.axis_size("ctx")
    d = lax.axis_index("ctx")
    layers, rows, q_cols = queries.shape
    assert n == KVH * layers
    kv_cols = draft_keys.shape[2]
    local_len = key_cache.shape[1]
    trees = ancestors.shape[0]
    heads_here = H // n
    score_scale = 1.0 / math.sqrt(DH)
    own = d % layers
    swap = [(s, s ^ 1) for s in range(n)]

    packed = jnp.concatenate([queries, draft_keys, draft_values], axis=2)
    mine_now = lax.dynamic_index_in_dim(packed, own, 0, keepdims=False)
    partner = lax.ppermute(lax.dynamic_index_in_dim(packed, 1 - own, 0, keepdims=False), "ctx", swap)
    first = jnp.where(own == 0, mine_now, partner)
    second = jnp.where(own == 0, partner, mine_now)

    keys_out = jnp.transpose(key_cache.reshape(layers, local_len, KVH, DH), (2, 0, 1, 3))
    values_out = jnp.transpose(value_cache.reshape(layers, local_len, KVH, DH), (2, 0, 3, 1))
    kv = jnp.stack([keys_out, values_out], 2).reshape(n, 2, local_len, DH)
    blocks = lax.all_to_all(kv, "ctx", 0, 0, tiled=True)

    tree_keep = (
        jnp.eye(trees, dtype=jnp.int32)[:, None, :, None] * ancestors[:, :, None, :]
    ).reshape(rows, rows)
    pair_heads = 2 * heads_here
    query_heads = jnp.concatenate(
        [first[:, :q_cols].reshape(rows, heads_here, DH), second[:, :q_cols].reshape(rows, heads_here, DH)], 1
    )
    q_rows = jnp.transpose(query_heads, (1, 0, 2)).reshape(pair_heads * rows, DH)
    draft_k = jnp.concatenate([first[:, q_cols:q_cols + kv_cols], second[:, q_cols:q_cols + kv_cols]], 1)
    draft_v = jnp.concatenate([first[:, q_cols + kv_cols:], second[:, q_cols + kv_cols:]], 1)
    tree_cols = jnp.tile(jnp.transpose(tree_keep), (1, pair_heads))
    done = attend(context_length, q_rows, blocks, draft_k, jnp.transpose(draft_v), tree_cols)
    done = jnp.transpose(done.reshape(DH, 2, heads_here, rows), (1, 2, 3, 0))
    keep = jnp.where(own == 0, done[0], done[1])
    got = lax.ppermute(jnp.where(own == 0, done[1], done[0]), "ctx", swap)
    keep = jnp.transpose(keep, (1, 0, 2)).reshape(rows, heads_here * DH)
    got = jnp.transpose(got, (1, 0, 2)).reshape(rows, heads_here * DH)
    return jnp.stack([jnp.where(own == 0, keep, got), jnp.where(own == 0, got, keep)])


def solution(mesh):
    placed = (
        P("req", None, "ctx"),
        P("req", "ctx", None),
        P("req", "ctx", None),
        P("req", None, "ctx"),
        P("req", None, "ctx"),
        P("req", None, None),
        P("req"),
    )
    return jax.shard_map(
        body, mesh=mesh, in_specs=placed, out_specs=P("req", None, "ctx"), check_vma=False
    )
```

```python
import math

import jax
import jax.numpy as jnp
from jax import lax
from jax.experimental import pallas as pl
from jax.experimental.pallas import tpu as pltpu
from jax.sharding import PartitionSpec as P

H = 64
KVH = 8
DH = 128


masked_score = -1e30


def send_target(s, j, n):
    return (s + j) % n if (s + j) % 2 == 0 else (s - j) % n


def blocks_partial(query_heads, block_keys, block_values, draft_k, draft_v, cache_keep, draft_keep, score_scale):
    scores = (
        jnp.einsum("qhd,jpd->hqjp", query_heads, block_keys, preferred_element_type=jnp.float32)
        * score_scale
    )
    draft_scores = (
        jnp.einsum("qhd,td->hqt", query_heads, draft_k, preferred_element_type=jnp.float32)
        * score_scale
    )
    scores = jnp.where(cache_keep[None, None], scores, masked_score)
    draft_scores = jnp.where(draft_keep[None], draft_scores[:, :, None, :], masked_score)
    top_score = jnp.maximum(jnp.max(scores, -1), jnp.max(draft_scores, -1))
    shift_by = jnp.where(top_score > -1e29, top_score, 0.0)
    cache_weight = jnp.exp(scores - shift_by[..., None])
    draft_weight = jnp.exp(draft_scores - shift_by[..., None])
    total = jnp.sum(cache_weight, -1) + jnp.sum(draft_weight, -1)
    weighted = jnp.einsum(
        "hqjp,jpd->hqjd",
        cache_weight.astype(jnp.bfloat16),
        block_values,
        preferred_element_type=jnp.float32,
    )
    weighted = weighted + jnp.einsum(
        "hqjt,td->hqjd",
        draft_weight.astype(jnp.bfloat16),
        draft_v,
        preferred_element_type=jnp.float32,
    )
    alive = total > 0.0
    safe_total = jnp.where(alive, total, 1.0)
    output = lax.reduce_precision(
        jnp.where(alive[..., None], weighted / safe_total[..., None], 0.0), exponent_bits=8, mantissa_bits=7
    )
    lse = jnp.where(alive, top_score + jnp.log(safe_total), masked_score)
    top = jnp.max(lse, -1)
    factor = jnp.where(lse > -1e29, jnp.exp(lse - top[..., None]), 0.0)
    return top, jnp.sum(factor, -1), jnp.sum(factor[..., None] * output, 2)


def _dot(a, b, dims):
    return lax.dot_general(a, b, dims, preferred_element_type=jnp.float32)


def attend_kernel(len_ref, q_ref, kv_ref, dk_ref, dvt_ref, tree_ref, o_ref, out_sc, lse_sc):
    blocks, _, block_len, _ = kv_ref.shape
    score_scale = 1.0 / math.sqrt(DH)
    nt = (((1,), (1,)), ((), ()))
    nn = (((1,), (0,)), ((), ()))
    q = q_ref[...]
    ctx_len = len_ref[0]
    all_keys = kv_ref[:, 0].reshape(blocks * block_len, DH)
    all_scores = _dot(all_keys, q, nt) * score_scale
    pos = lax.broadcasted_iota(jnp.int32, all_scores.shape, 0)
    all_scores = jnp.where(pos < ctx_len, all_scores, masked_score)
    for j in range(blocks):
        scores = all_scores[j * block_len:(j + 1) * block_len]
        top = jnp.max(scores, axis=0, keepdims=True)
        if j == 0:
            draft = _dot(dk_ref[...], q, nt) * score_scale
            draft = jnp.where(tree_ref[...] > 0, draft, masked_score)
            top = jnp.maximum(top, jnp.max(draft, axis=0, keepdims=True))
        shift = jnp.where(top > -1e29, top, 0.0)
        weight = jnp.exp(scores - shift)
        total = jnp.sum(weight, axis=0, keepdims=True)
        acc = _dot(kv_ref[j, 1], weight.astype(jnp.bfloat16), nn)
        if j == 0:
            draft_weight = jnp.exp(draft - shift)
            total = total + jnp.sum(draft_weight, axis=0, keepdims=True)
            acc = acc + _dot(dvt_ref[...], draft_weight.astype(jnp.bfloat16), nn)
        alive = total > 0.0
        safe = jnp.where(alive, total, 1.0)
        out_sc[j] = jnp.where(alive, acc / safe, 0.0).astype(jnp.bfloat16).astype(jnp.float32)
        lse_sc[j:j + 1, :] = jnp.where(alive, top + jnp.log(safe), masked_score)
    lse = lse_sc[...]
    overall = jnp.max(lse, axis=0, keepdims=True)
    factor = jnp.exp(lse - overall)
    weighted = factor[0:1] * out_sc[0]
    for j in range(1, blocks):
        weighted = weighted + factor[j:j + 1] * out_sc[j]
    o_ref[...] = weighted / jnp.sum(factor, axis=0, keepdims=True)


def attend(context_length, q_rows, blocks_kv, draft_k, draft_vt, tree_cols):
    rows = q_rows.shape[0]
    blocks = blocks_kv.shape[0]
    vmem = pl.BlockSpec(memory_space=pltpu.VMEM)
    return pl.pallas_call(
        attend_kernel,
        out_shape=jax.ShapeDtypeStruct((DH, rows), jnp.float32),
        in_specs=[pl.BlockSpec(memory_space=pltpu.SMEM)] + [vmem] * 5,
        out_specs=vmem,
        scratch_shapes=[pltpu.VMEM((blocks, DH, rows), jnp.float32), pltpu.VMEM((blocks, rows), jnp.float32)],
    )(context_length, q_rows, blocks_kv, draft_k, draft_vt, tree_cols)


def body(queries, key_cache, value_cache, draft_keys, draft_values, ancestors, context_length):
    n = lax.axis_size("ctx")
    d = lax.axis_index("ctx")
    layers, rows, q_cols = queries.shape
    assert n == KVH * layers
    kv_cols = draft_keys.shape[2]
    local_len = key_cache.shape[1]
    trees = ancestors.shape[0]
    heads_here = H // n
    score_scale = 1.0 / math.sqrt(DH)
    own = d % layers
    swap = [(s, s ^ 1) for s in range(n)]

    packed = jnp.concatenate([queries, draft_keys, draft_values], axis=2)
    mine_now = lax.dynamic_index_in_dim(packed, own, 0, keepdims=False)
    partner = lax.ppermute(lax.dynamic_index_in_dim(packed, 1 - own, 0, keepdims=False), "ctx", swap)
    first = jnp.where(own == 0, mine_now, partner)
    second = jnp.where(own == 0, partner, mine_now)

    keys_out = jnp.transpose(key_cache.reshape(layers, local_len, KVH, DH), (2, 0, 1, 3))
    values_out = jnp.transpose(value_cache.reshape(layers, local_len, KVH, DH), (2, 0, 3, 1))
    kv = jnp.stack([keys_out, values_out], 2).reshape(n, 2, local_len, DH)
    blocks = lax.all_to_all(kv, "ctx", 0, 0, tiled=True)

    tree_keep = (
        jnp.eye(trees, dtype=jnp.int32)[:, None, :, None] * ancestors[:, :, None, :]
    ).reshape(rows, rows)
    pair_heads = 2 * heads_here
    query_heads = jnp.concatenate(
        [first[:, :q_cols].reshape(rows, heads_here, DH), second[:, :q_cols].reshape(rows, heads_here, DH)], 1
    )
    q_rows = jnp.transpose(query_heads, (1, 0, 2)).reshape(pair_heads * rows, DH)
    draft_k = jnp.concatenate([first[:, q_cols:q_cols + kv_cols], second[:, q_cols:q_cols + kv_cols]], 1)
    draft_v = jnp.concatenate([first[:, q_cols + kv_cols:], second[:, q_cols + kv_cols:]], 1)
    tree_cols = jnp.tile(jnp.transpose(tree_keep), (1, pair_heads))
    done = attend(context_length, q_rows, blocks, draft_k, jnp.transpose(draft_v), tree_cols)
    done = jnp.transpose(done.reshape(DH, 2, heads_here, rows), (1, 2, 3, 0))
    keep = jnp.where(own == 0, done[0], done[1])
    got = lax.ppermute(jnp.where(own == 0, done[1], done[0]), "ctx", swap)
    keep = jnp.transpose(keep, (1, 0, 2)).reshape(rows, heads_here * DH)
    got = jnp.transpose(got, (1, 0, 2)).reshape(rows, heads_here * DH)
    return jnp.stack([jnp.where(own == 0, keep, got), jnp.where(own == 0, got, keep)])


def solution(mesh):
    placed = (
        P("req", None, "ctx"),
        P("req", "ctx", None),
        P("req", "ctx", None),
        P("req", None, "ctx"),
        P("req", None, "ctx"),
        P("req", None, None),
        P("req"),
    )
    return jax.shard_map(
        body, mesh=mesh, in_specs=placed, out_specs=P("req", None, "ctx"), check_vma=False
    )
```

```python
import math

import jax
import jax.numpy as jnp
from jax import lax
from jax.experimental import pallas as pl
from jax.experimental.pallas import tpu as pltpu
from jax.sharding import PartitionSpec as P

H = 64
KVH = 8
DH = 128


masked_score = -1e30


def send_target(s, j, n):
    return (s + j) % n if (s + j) % 2 == 0 else (s - j) % n


def blocks_partial(query_heads, block_keys, block_values, draft_k, draft_v, cache_keep, draft_keep, score_scale):
    scores = (
        jnp.einsum("qhd,jpd->hqjp", query_heads, block_keys, preferred_element_type=jnp.float32)
        * score_scale
    )
    draft_scores = (
        jnp.einsum("qhd,td->hqt", query_heads, draft_k, preferred_element_type=jnp.float32)
        * score_scale
    )
    scores = jnp.where(cache_keep[None, None], scores, masked_score)
    draft_scores = jnp.where(draft_keep[None], draft_scores[:, :, None, :], masked_score)
    top_score = jnp.maximum(jnp.max(scores, -1), jnp.max(draft_scores, -1))
    shift_by = jnp.where(top_score > -1e29, top_score, 0.0)
    cache_weight = jnp.exp(scores - shift_by[..., None])
    draft_weight = jnp.exp(draft_scores - shift_by[..., None])
    total = jnp.sum(cache_weight, -1) + jnp.sum(draft_weight, -1)
    weighted = jnp.einsum(
        "hqjp,jpd->hqjd",
        cache_weight.astype(jnp.bfloat16),
        block_values,
        preferred_element_type=jnp.float32,
    )
    weighted = weighted + jnp.einsum(
        "hqjt,td->hqjd",
        draft_weight.astype(jnp.bfloat16),
        draft_v,
        preferred_element_type=jnp.float32,
    )
    alive = total > 0.0
    safe_total = jnp.where(alive, total, 1.0)
    output = lax.reduce_precision(
        jnp.where(alive[..., None], weighted / safe_total[..., None], 0.0), exponent_bits=8, mantissa_bits=7
    )
    lse = jnp.where(alive, top_score + jnp.log(safe_total), masked_score)
    top = jnp.max(lse, -1)
    factor = jnp.where(lse > -1e29, jnp.exp(lse - top[..., None]), 0.0)
    return top, jnp.sum(factor, -1), jnp.sum(factor[..., None] * output, 2)


def _dot(a, b, dims):
    return lax.dot_general(a, b, dims, preferred_element_type=jnp.float32)


def attend_kernel(len_ref, q_ref, kv_ref, dk_ref, dvt_ref, tree_ref, o_ref, out_sc, lse_sc):
    blocks, _, block_len, _ = kv_ref.shape
    score_scale = 1.0 / math.sqrt(DH)
    nt = (((1,), (1,)), ((), ()))
    nn = (((1,), (0,)), ((), ()))
    q = q_ref[...]
    ctx_len = len_ref[0]
    all_keys = kv_ref[:, 0].reshape(blocks * block_len, DH)
    all_scores = _dot(all_keys, q, nt) * score_scale
    pos = lax.broadcasted_iota(jnp.int32, all_scores.shape, 0)
    all_scores = jnp.where(pos < ctx_len, all_scores, masked_score)
    for j in range(blocks):
        scores = all_scores[j * block_len:(j + 1) * block_len]
        top = jnp.max(scores, axis=0, keepdims=True)
        if j == 0:
            draft = _dot(dk_ref[...], q, nt) * score_scale
            draft = jnp.where(tree_ref[...] > 0, draft, masked_score)
            top = jnp.maximum(top, jnp.max(draft, axis=0, keepdims=True))
        shift = jnp.where(top > -1e29, top, 0.0)
        weight = jnp.exp(scores - shift)
        total = jnp.sum(weight, axis=0, keepdims=True)
        acc = _dot(kv_ref[j, 1], weight.astype(jnp.bfloat16), nn)
        if j == 0:
            draft_weight = jnp.exp(draft - shift)
            total = total + jnp.sum(draft_weight, axis=0, keepdims=True)
            acc = acc + _dot(dvt_ref[...], draft_weight.astype(jnp.bfloat16), nn)
        alive = total > 0.0
        safe = jnp.where(alive, total, 1.0)
        out_sc[j] = jnp.where(alive, acc / safe, 0.0).astype(jnp.bfloat16).astype(jnp.float32)
        lse_sc[j:j + 1, :] = jnp.where(alive, top + jnp.log(safe), masked_score)
    lse = lse_sc[...]
    overall = jnp.max(lse, axis=0, keepdims=True)
    factor = jnp.exp(lse - overall)
    weighted = factor[0:1] * out_sc[0]
    for j in range(1, blocks):
        weighted = weighted + factor[j:j + 1] * out_sc[j]
    o_ref[...] = weighted / jnp.sum(factor, axis=0, keepdims=True)


def attend(context_length, q_rows, blocks_kv, draft_k, draft_vt, tree_cols):
    rows = q_rows.shape[0]
    blocks = blocks_kv.shape[0]
    vmem = pl.BlockSpec(memory_space=pltpu.VMEM)
    return pl.pallas_call(
        attend_kernel,
        out_shape=jax.ShapeDtypeStruct((DH, rows), jnp.float32),
        in_specs=[pl.BlockSpec(memory_space=pltpu.SMEM)] + [vmem] * 5,
        out_specs=vmem,
        scratch_shapes=[pltpu.VMEM((blocks, DH, rows), jnp.float32), pltpu.VMEM((blocks, rows), jnp.float32)],
    )(context_length, q_rows, blocks_kv, draft_k, draft_vt, tree_cols)


def body(queries, key_cache, value_cache, draft_keys, draft_values, ancestors, context_length):
    n = lax.axis_size("ctx")
    d = lax.axis_index("ctx")
    layers, rows, q_cols = queries.shape
    assert n == KVH * layers
    kv_cols = draft_keys.shape[2]
    local_len = key_cache.shape[1]
    trees = ancestors.shape[0]
    heads_here = H // n
    score_scale = 1.0 / math.sqrt(DH)
    own = d % layers
    swap = [(s, s ^ 1) for s in range(n)]

    packed = jnp.concatenate([queries, draft_keys, draft_values], axis=2)
    mine_now = lax.dynamic_index_in_dim(packed, own, 0, keepdims=False)
    partner = lax.ppermute(lax.dynamic_index_in_dim(packed, 1 - own, 0, keepdims=False), "ctx", swap)
    first = jnp.where(own == 0, mine_now, partner)
    second = jnp.where(own == 0, partner, mine_now)

    keys_out = jnp.transpose(key_cache.reshape(layers, local_len, KVH, DH), (2, 0, 1, 3))
    values_out = jnp.transpose(value_cache.reshape(layers, local_len, KVH, DH), (2, 0, 3, 1))
    kv = jnp.stack([keys_out, values_out], 2).reshape(n, 2, local_len, DH)
    blocks = lax.all_to_all(kv, "ctx", 0, 0, tiled=True)

    tree_keep = (
        jnp.eye(trees, dtype=jnp.int32)[:, None, :, None] * ancestors[:, :, None, :]
    ).reshape(rows, rows)
    own_q = jnp.transpose(mine_now[:, :q_cols].reshape(rows, heads_here, DH), (1, 0, 2))
    other_q = jnp.transpose(partner[:, :q_cols].reshape(rows, heads_here, DH), (1, 0, 2))
    draft_k = jnp.concatenate([first[:, q_cols:q_cols + kv_cols], second[:, q_cols:q_cols + kv_cols]], 1)
    draft_vt = jnp.transpose(jnp.concatenate([first[:, q_cols + kv_cols:], second[:, q_cols + kv_cols:]], 1))
    tree_cols = jnp.tile(jnp.transpose(tree_keep), (1, heads_here))
    give = attend(context_length, other_q.reshape(heads_here * rows, DH), blocks, draft_k, draft_vt, tree_cols)
    got = lax.ppermute(give, "ctx", swap)
    keep = attend(context_length, own_q.reshape(heads_here * rows, DH), blocks, draft_k, draft_vt, tree_cols)
    keep = jnp.transpose(keep.reshape(DH, heads_here, rows), (1, 2, 0))
    got = jnp.transpose(got.reshape(DH, heads_here, rows), (1, 2, 0))
    keep = jnp.transpose(keep, (1, 0, 2)).reshape(rows, heads_here * DH)
    got = jnp.transpose(got, (1, 0, 2)).reshape(rows, heads_here * DH)
    return jnp.stack([jnp.where(own == 0, keep, got), jnp.where(own == 0, got, keep)])


def solution(mesh):
    placed = (
        P("req", None, "ctx"),
        P("req", "ctx", None),
        P("req", "ctx", None),
        P("req", None, "ctx"),
        P("req", None, "ctx"),
        P("req", None, None),
        P("req"),
    )
    return jax.shard_map(
        body, mesh=mesh, in_specs=placed, out_specs=P("req", None, "ctx"), check_vma=False
    )
```

```python
import math

import jax
import jax.numpy as jnp
from jax import lax
from jax.experimental import pallas as pl
from jax.experimental.pallas import tpu as pltpu
from jax.sharding import PartitionSpec as P

H = 64
KVH = 8
DH = 128


masked_score = -1e30


def send_target(s, j, n):
    return (s + j) % n if (s + j) % 2 == 0 else (s - j) % n


def blocks_partial(query_heads, block_keys, block_values, draft_k, draft_v, cache_keep, draft_keep, score_scale):
    scores = (
        jnp.einsum("qhd,jpd->hqjp", query_heads, block_keys, preferred_element_type=jnp.float32)
        * score_scale
    )
    draft_scores = (
        jnp.einsum("qhd,td->hqt", query_heads, draft_k, preferred_element_type=jnp.float32)
        * score_scale
    )
    scores = jnp.where(cache_keep[None, None], scores, masked_score)
    draft_scores = jnp.where(draft_keep[None], draft_scores[:, :, None, :], masked_score)
    top_score = jnp.maximum(jnp.max(scores, -1), jnp.max(draft_scores, -1))
    shift_by = jnp.where(top_score > -1e29, top_score, 0.0)
    cache_weight = jnp.exp(scores - shift_by[..., None])
    draft_weight = jnp.exp(draft_scores - shift_by[..., None])
    total = jnp.sum(cache_weight, -1) + jnp.sum(draft_weight, -1)
    weighted = jnp.einsum(
        "hqjp,jpd->hqjd",
        cache_weight.astype(jnp.bfloat16),
        block_values,
        preferred_element_type=jnp.float32,
    )
    weighted = weighted + jnp.einsum(
        "hqjt,td->hqjd",
        draft_weight.astype(jnp.bfloat16),
        draft_v,
        preferred_element_type=jnp.float32,
    )
    alive = total > 0.0
    safe_total = jnp.where(alive, total, 1.0)
    output = lax.reduce_precision(
        jnp.where(alive[..., None], weighted / safe_total[..., None], 0.0), exponent_bits=8, mantissa_bits=7
    )
    lse = jnp.where(alive, top_score + jnp.log(safe_total), masked_score)
    top = jnp.max(lse, -1)
    factor = jnp.where(lse > -1e29, jnp.exp(lse - top[..., None]), 0.0)
    return top, jnp.sum(factor, -1), jnp.sum(factor[..., None] * output, 2)


def _dot(a, b, dims):
    return lax.dot_general(a, b, dims, preferred_element_type=jnp.float32)


def attend_kernel(len_ref, q_ref, kv_ref, dk_ref, dvt_ref, tree_ref, o_ref, out_sc, lse_sc):
    blocks, _, block_len, _ = kv_ref.shape
    score_scale = 1.0 / math.sqrt(DH)
    nt = (((1,), (1,)), ((), ()))
    tn = (((0,), (0,)), ((), ()))
    q = q_ref[...]
    ctx_len = len_ref[0]
    all_keys = kv_ref[:, 0].reshape(blocks * block_len, DH)
    all_scores = _dot(all_keys, q, nt) * score_scale
    pos = lax.broadcasted_iota(jnp.int32, all_scores.shape, 0)
    all_scores = jnp.where(pos < ctx_len, all_scores, masked_score)
    for j in range(blocks):
        scores = all_scores[j * block_len:(j + 1) * block_len]
        top = jnp.max(scores, axis=0, keepdims=True)
        if j == 0:
            draft = _dot(dk_ref[...], q, nt) * score_scale
            draft = jnp.where(tree_ref[...] > 0, draft, masked_score)
            top = jnp.maximum(top, jnp.max(draft, axis=0, keepdims=True))
        shift = jnp.where(top > -1e29, top, 0.0)
        weight = jnp.exp(scores - shift)
        total = jnp.sum(weight, axis=0, keepdims=True)
        acc = _dot(kv_ref[j, 1], weight.astype(jnp.bfloat16), tn)
        if j == 0:
            draft_weight = jnp.exp(draft - shift)
            total = total + jnp.sum(draft_weight, axis=0, keepdims=True)
            acc = acc + _dot(dvt_ref[...], draft_weight.astype(jnp.bfloat16), tn)
        alive = total > 0.0
        safe = jnp.where(alive, total, 1.0)
        out_sc[j] = jnp.where(alive, acc / safe, 0.0).astype(jnp.bfloat16).astype(jnp.float32)
        lse_sc[j:j + 1, :] = jnp.where(alive, top + jnp.log(safe), masked_score)
    lse = lse_sc[...]
    overall = jnp.max(lse, axis=0, keepdims=True)
    factor = jnp.exp(lse - overall)
    weighted = factor[0:1] * out_sc[0]
    for j in range(1, blocks):
        weighted = weighted + factor[j:j + 1] * out_sc[j]
    o_ref[...] = weighted / jnp.sum(factor, axis=0, keepdims=True)


def attend(context_length, q_rows, blocks_kv, draft_k, draft_vt, tree_cols):
    rows = q_rows.shape[0]
    blocks = blocks_kv.shape[0]
    vmem = pl.BlockSpec(memory_space=pltpu.VMEM)
    return pl.pallas_call(
        attend_kernel,
        out_shape=jax.ShapeDtypeStruct((DH, rows), jnp.float32),
        in_specs=[pl.BlockSpec(memory_space=pltpu.SMEM)] + [vmem] * 5,
        out_specs=vmem,
        scratch_shapes=[pltpu.VMEM((blocks, DH, rows), jnp.float32), pltpu.VMEM((blocks, rows), jnp.float32)],
    )(context_length, q_rows, blocks_kv, draft_k, draft_vt, tree_cols)


def body(queries, key_cache, value_cache, draft_keys, draft_values, ancestors, context_length):
    n = lax.axis_size("ctx")
    d = lax.axis_index("ctx")
    layers, rows, q_cols = queries.shape
    assert n == KVH * layers
    kv_cols = draft_keys.shape[2]
    local_len = key_cache.shape[1]
    trees = ancestors.shape[0]
    heads_here = H // n
    score_scale = 1.0 / math.sqrt(DH)
    own = d % layers
    swap = [(s, s ^ 1) for s in range(n)]

    other = 1 - own
    swapped = [
        lax.ppermute(lax.dynamic_index_in_dim(a, other, 0, keepdims=False), "ctx", swap)
        for a in (queries, draft_keys, draft_values)
    ]
    mine_now = [lax.dynamic_index_in_dim(a, own, 0, keepdims=False) for a in (queries, draft_keys, draft_values)]
    first = [jnp.where(own == 0, a, b) for a, b in zip(mine_now, swapped)]
    second = [jnp.where(own == 0, b, a) for a, b in zip(mine_now, swapped)]

    keys_out = jnp.transpose(key_cache.reshape(layers, local_len, KVH, DH), (2, 0, 1, 3))
    values_out = jnp.transpose(value_cache.reshape(layers, local_len, KVH, DH), (2, 0, 1, 3))
    kv = jnp.stack([keys_out, values_out], 2).reshape(n, 2, local_len, DH)
    blocks = lax.all_to_all(kv, "ctx", 0, 0, tiled=True)

    tree_keep = (
        jnp.eye(trees, dtype=jnp.int32)[:, None, :, None] * ancestors[:, :, None, :]
    ).reshape(rows, rows)
    own_q = jnp.transpose(mine_now[0].reshape(rows, heads_here, DH), (1, 0, 2))
    other_q = jnp.transpose(swapped[0].reshape(rows, heads_here, DH), (1, 0, 2))
    draft_k = jnp.concatenate([first[1], second[1]], 1)
    draft_vt = jnp.concatenate([first[2], second[2]], 1)
    tree_cols = jnp.tile(jnp.transpose(tree_keep), (1, heads_here))
    give = attend(context_length, other_q.reshape(heads_here * rows, DH), blocks, draft_k, draft_vt, tree_cols)
    got = lax.ppermute(give, "ctx", swap)
    keep = attend(context_length, own_q.reshape(heads_here * rows, DH), blocks, draft_k, draft_vt, tree_cols)
    keep = jnp.transpose(keep.reshape(DH, heads_here, rows), (2, 1, 0)).reshape(1, rows, heads_here * DH)
    got = jnp.transpose(got.reshape(DH, heads_here, rows), (2, 1, 0)).reshape(1, rows, heads_here * DH)
    result = jnp.zeros((layers, rows, heads_here * DH), jnp.float32)
    result = lax.dynamic_update_slice(result, keep, (own, 0, 0))
    return lax.dynamic_update_slice(result, got, (other, 0, 0))

def solution(mesh):
    placed = (
        P("req", None, "ctx"),
        P("req", "ctx", None),
        P("req", "ctx", None),
        P("req", None, "ctx"),
        P("req", None, "ctx"),
        P("req", None, None),
        P("req"),
    )
    return jax.shard_map(
        body, mesh=mesh, in_specs=placed, out_specs=P("req", None, "ctx"), check_vma=False
    )
```

```python
import math

import jax
import jax.numpy as jnp
from jax import lax
from jax.experimental import pallas as pl
from jax.experimental.pallas import tpu as pltpu
from jax.sharding import PartitionSpec as P

H = 64
KVH = 8
DH = 128


masked_score = -1e30


def send_target(s, j, n):
    return (s + j) % n if (s + j) % 2 == 0 else (s - j) % n


def blocks_partial(query_heads, block_keys, block_values, draft_k, draft_v, cache_keep, draft_keep, score_scale):
    scores = (
        jnp.einsum("qhd,jpd->hqjp", query_heads, block_keys, preferred_element_type=jnp.float32)
        * score_scale
    )
    draft_scores = (
        jnp.einsum("qhd,td->hqt", query_heads, draft_k, preferred_element_type=jnp.float32)
        * score_scale
    )
    scores = jnp.where(cache_keep[None, None], scores, masked_score)
    draft_scores = jnp.where(draft_keep[None], draft_scores[:, :, None, :], masked_score)
    top_score = jnp.maximum(jnp.max(scores, -1), jnp.max(draft_scores, -1))
    shift_by = jnp.where(top_score > -1e29, top_score, 0.0)
    cache_weight = jnp.exp(scores - shift_by[..., None])
    draft_weight = jnp.exp(draft_scores - shift_by[..., None])
    total = jnp.sum(cache_weight, -1) + jnp.sum(draft_weight, -1)
    weighted = jnp.einsum(
        "hqjp,jpd->hqjd",
        cache_weight.astype(jnp.bfloat16),
        block_values,
        preferred_element_type=jnp.float32,
    )
    weighted = weighted + jnp.einsum(
        "hqjt,td->hqjd",
        draft_weight.astype(jnp.bfloat16),
        draft_v,
        preferred_element_type=jnp.float32,
    )
    alive = total > 0.0
    safe_total = jnp.where(alive, total, 1.0)
    output = lax.reduce_precision(
        jnp.where(alive[..., None], weighted / safe_total[..., None], 0.0), exponent_bits=8, mantissa_bits=7
    )
    lse = jnp.where(alive, top_score + jnp.log(safe_total), masked_score)
    top = jnp.max(lse, -1)
    factor = jnp.where(lse > -1e29, jnp.exp(lse - top[..., None]), 0.0)
    return top, jnp.sum(factor, -1), jnp.sum(factor[..., None] * output, 2)


def _dot(a, b, dims):
    return lax.dot_general(a, b, dims, preferred_element_type=jnp.float32)


def attend_kernel(len_ref, q_ref, kv_ref, dk_ref, dvt_ref, tree_ref, o_ref, out_sc, lse_sc):
    blocks, _, block_len, _ = kv_ref.shape
    score_scale = 1.0 / math.sqrt(DH)
    nt = (((1,), (1,)), ((), ()))
    tn = (((0,), (0,)), ((), ()))
    q = q_ref[...]
    ctx_len = len_ref[0]
    all_keys = kv_ref[:, 0].reshape(blocks * block_len, DH)
    all_scores = _dot(all_keys, q, nt) * score_scale
    pos = lax.broadcasted_iota(jnp.int32, all_scores.shape, 0)
    all_scores = jnp.where(pos < ctx_len, all_scores, masked_score)
    for j in range(blocks):
        scores = all_scores[j * block_len:(j + 1) * block_len]
        top = jnp.max(scores, axis=0, keepdims=True)
        if j == 0:
            draft = _dot(dk_ref[...], q, nt) * score_scale
            draft = jnp.where(tree_ref[...] > 0, draft, masked_score)
            top = jnp.maximum(top, jnp.max(draft, axis=0, keepdims=True))
        shift = jnp.where(top > -1e29, top, 0.0)
        weight = jnp.exp(scores - shift)
        total = jnp.sum(weight, axis=0, keepdims=True)
        acc = _dot(kv_ref[j, 1], weight.astype(jnp.bfloat16), tn)
        if j == 0:
            draft_weight = jnp.exp(draft - shift)
            total = total + jnp.sum(draft_weight, axis=0, keepdims=True)
            acc = acc + _dot(dvt_ref[...], draft_weight.astype(jnp.bfloat16), tn)
        alive = total > 0.0
        safe = jnp.where(alive, total, 1.0)
        out_sc[j] = jnp.where(alive, acc / safe, 0.0).astype(jnp.bfloat16).astype(jnp.float32)
        lse_sc[j:j + 1, :] = jnp.where(alive, top + jnp.log(safe), masked_score)
    lse = lse_sc[...]
    overall = jnp.max(lse, axis=0, keepdims=True)
    factor = jnp.exp(lse - overall)
    weighted = factor[0:1] * out_sc[0]
    for j in range(1, blocks):
        weighted = weighted + factor[j:j + 1] * out_sc[j]
    o_ref[...] = weighted / jnp.sum(factor, axis=0, keepdims=True)


def attend(context_length, q_rows, blocks_kv, draft_k, draft_vt, tree_cols):
    rows = q_rows.shape[0]
    blocks = blocks_kv.shape[0]
    vmem = pl.BlockSpec(memory_space=pltpu.VMEM)
    operands = [pltpu.with_memory_space_constraint(a, pltpu.VMEM)
                for a in (q_rows, blocks_kv, draft_k, draft_vt, tree_cols)]
    return pl.pallas_call(
        attend_kernel,
        out_shape=jax.ShapeDtypeStruct((DH, rows), jnp.float32),
        in_specs=[pl.BlockSpec(memory_space=pltpu.SMEM)] + [vmem] * 5,
        out_specs=vmem,
        scratch_shapes=[pltpu.VMEM((blocks, DH, rows), jnp.float32), pltpu.VMEM((blocks, rows), jnp.float32)],
    )(context_length, *operands)


def body(queries, key_cache, value_cache, draft_keys, draft_values, ancestors, context_length):
    n = lax.axis_size("ctx")
    d = lax.axis_index("ctx")
    layers, rows, q_cols = queries.shape
    assert n == KVH * layers
    kv_cols = draft_keys.shape[2]
    local_len = key_cache.shape[1]
    trees = ancestors.shape[0]
    heads_here = H // n
    score_scale = 1.0 / math.sqrt(DH)
    own = d % layers
    swap = [(s, s ^ 1) for s in range(n)]

    other = 1 - own
    swapped = [
        lax.ppermute(lax.dynamic_index_in_dim(a, other, 0, keepdims=False), "ctx", swap)
        for a in (queries, draft_keys, draft_values)
    ]
    mine_now = [lax.dynamic_index_in_dim(a, own, 0, keepdims=False) for a in (queries, draft_keys, draft_values)]
    first = [jnp.where(own == 0, a, b) for a, b in zip(mine_now, swapped)]
    second = [jnp.where(own == 0, b, a) for a, b in zip(mine_now, swapped)]

    keys_out = jnp.transpose(key_cache.reshape(layers, local_len, KVH, DH), (2, 0, 1, 3))
    values_out = jnp.transpose(value_cache.reshape(layers, local_len, KVH, DH), (2, 0, 1, 3))
    kv = jnp.stack([keys_out, values_out], 2).reshape(n, 2, local_len, DH)
    blocks = lax.all_to_all(kv, "ctx", 0, 0, tiled=True)

    tree_keep = (
        jnp.eye(trees, dtype=jnp.int32)[:, None, :, None] * ancestors[:, :, None, :]
    ).reshape(rows, rows)
    own_q = jnp.transpose(mine_now[0].reshape(rows, heads_here, DH), (1, 0, 2))
    other_q = jnp.transpose(swapped[0].reshape(rows, heads_here, DH), (1, 0, 2))
    draft_k = jnp.concatenate([first[1], second[1]], 1)
    draft_vt = jnp.concatenate([first[2], second[2]], 1)
    tree_cols = jnp.tile(jnp.transpose(tree_keep), (1, heads_here))
    give = attend(context_length, other_q.reshape(heads_here * rows, DH), blocks, draft_k, draft_vt, tree_cols)
    got = lax.ppermute(give, "ctx", swap)
    keep = attend(context_length, own_q.reshape(heads_here * rows, DH), blocks, draft_k, draft_vt, tree_cols)
    keep = jnp.transpose(keep.reshape(DH, heads_here, rows), (2, 1, 0)).reshape(1, rows, heads_here * DH)
    got = jnp.transpose(got.reshape(DH, heads_here, rows), (2, 1, 0)).reshape(1, rows, heads_here * DH)
    result = jnp.zeros((layers, rows, heads_here * DH), jnp.float32)
    result = lax.dynamic_update_slice(result, keep, (own, 0, 0))
    return lax.dynamic_update_slice(result, got, (other, 0, 0))

def solution(mesh):
    placed = (
        P("req", None, "ctx"),
        P("req", "ctx", None),
        P("req", "ctx", None),
        P("req", None, "ctx"),
        P("req", None, "ctx"),
        P("req", None, None),
        P("req"),
    )
    return jax.shard_map(
        body, mesh=mesh, in_specs=placed, out_specs=P("req", None, "ctx"), check_vma=False
    )
```

```python
import math

import jax
import jax.numpy as jnp
from jax import lax
from jax.experimental import pallas as pl
from jax.experimental.pallas import tpu as pltpu
from jax.sharding import PartitionSpec as P

H = 64
KVH = 8
DH = 128


masked_score = -1e30


def send_target(s, j, n):
    return (s + j) % n if (s + j) % 2 == 0 else (s - j) % n


def blocks_partial(query_heads, block_keys, block_values, draft_k, draft_v, cache_keep, draft_keep, score_scale):
    scores = (
        jnp.einsum("qhd,jpd->hqjp", query_heads, block_keys, preferred_element_type=jnp.float32)
        * score_scale
    )
    draft_scores = (
        jnp.einsum("qhd,td->hqt", query_heads, draft_k, preferred_element_type=jnp.float32)
        * score_scale
    )
    scores = jnp.where(cache_keep[None, None], scores, masked_score)
    draft_scores = jnp.where(draft_keep[None], draft_scores[:, :, None, :], masked_score)
    top_score = jnp.maximum(jnp.max(scores, -1), jnp.max(draft_scores, -1))
    shift_by = jnp.where(top_score > -1e29, top_score, 0.0)
    cache_weight = jnp.exp(scores - shift_by[..., None])
    draft_weight = jnp.exp(draft_scores - shift_by[..., None])
    total = jnp.sum(cache_weight, -1) + jnp.sum(draft_weight, -1)
    weighted = jnp.einsum(
        "hqjp,jpd->hqjd",
        cache_weight.astype(jnp.bfloat16),
        block_values,
        preferred_element_type=jnp.float32,
    )
    weighted = weighted + jnp.einsum(
        "hqjt,td->hqjd",
        draft_weight.astype(jnp.bfloat16),
        draft_v,
        preferred_element_type=jnp.float32,
    )
    alive = total > 0.0
    safe_total = jnp.where(alive, total, 1.0)
    output = lax.reduce_precision(
        jnp.where(alive[..., None], weighted / safe_total[..., None], 0.0), exponent_bits=8, mantissa_bits=7
    )
    lse = jnp.where(alive, top_score + jnp.log(safe_total), masked_score)
    top = jnp.max(lse, -1)
    factor = jnp.where(lse > -1e29, jnp.exp(lse - top[..., None]), 0.0)
    return top, jnp.sum(factor, -1), jnp.sum(factor[..., None] * output, 2)


def _dot(a, b, dims):
    return lax.dot_general(a, b, dims, preferred_element_type=jnp.float32)


def attend_kernel(len_ref, q_ref, kv_ref, dk_ref, dvt_ref, tree_ref, o_ref, out_sc, lse_sc):
    blocks, _, block_len, _ = kv_ref.shape
    score_scale = 1.0 / math.sqrt(DH)
    nt = (((1,), (1,)), ((), ()))
    tn = (((0,), (0,)), ((), ()))
    q = q_ref[...]
    ctx_len = len_ref[0]
    all_keys = kv_ref[:, 0].reshape(blocks * block_len, DH)
    all_scores = _dot(all_keys, q, nt) * score_scale
    pos = lax.broadcasted_iota(jnp.int32, all_scores.shape, 0)
    all_scores = jnp.where(pos < ctx_len, all_scores, masked_score)
    for j in range(blocks):
        scores = all_scores[j * block_len:(j + 1) * block_len]
        top = jnp.max(scores, axis=0, keepdims=True)
        if j == 0:
            draft = _dot(dk_ref[...], q, nt) * score_scale
            draft = jnp.where(tree_ref[...] > 0, draft, masked_score)
            top = jnp.maximum(top, jnp.max(draft, axis=0, keepdims=True))
        shift = jnp.where(top > -1e29, top, 0.0)
        weight = jnp.exp(scores - shift)
        total = jnp.sum(weight, axis=0, keepdims=True)
        acc = _dot(kv_ref[j, 1], weight.astype(jnp.bfloat16), tn)
        if j == 0:
            draft_weight = jnp.exp(draft - shift)
            total = total + jnp.sum(draft_weight, axis=0, keepdims=True)
            acc = acc + _dot(dvt_ref[...], draft_weight.astype(jnp.bfloat16), tn)
        alive = total > 0.0
        safe = jnp.where(alive, total, 1.0)
        out_sc[j] = jnp.where(alive, acc / safe, 0.0).astype(jnp.bfloat16).astype(jnp.float32)
        lse_sc[j:j + 1, :] = jnp.where(alive, top + jnp.log(safe), masked_score)
    lse = lse_sc[...]
    overall = jnp.max(lse, axis=0, keepdims=True)
    factor = jnp.exp(lse - overall)
    weighted = factor[0:1] * out_sc[0]
    for j in range(1, blocks):
        weighted = weighted + factor[j:j + 1] * out_sc[j]
    final = jnp.transpose(weighted / jnp.sum(factor, axis=0, keepdims=True))
    rows = o_ref.shape[0]
    for i in range(o_ref.shape[1] // DH):
        o_ref[:, i * DH:(i + 1) * DH] = final[i * rows:(i + 1) * rows, :]


def attend(context_length, q_rows, blocks_kv, draft_k, draft_vt, tree_cols, heads):
    rows = q_rows.shape[0]
    blocks = blocks_kv.shape[0]
    vmem = pl.BlockSpec(memory_space=pltpu.VMEM)
    operands = [pltpu.with_memory_space_constraint(a, pltpu.VMEM)
                for a in (q_rows, blocks_kv, draft_k, draft_vt, tree_cols)]
    return pl.pallas_call(
        attend_kernel,
        out_shape=jax.ShapeDtypeStruct((rows // heads, heads * DH), jnp.float32),
        in_specs=[pl.BlockSpec(memory_space=pltpu.SMEM)] + [vmem] * 5,
        out_specs=vmem,
        scratch_shapes=[pltpu.VMEM((blocks, DH, rows), jnp.float32), pltpu.VMEM((blocks, rows), jnp.float32)],
    )(context_length, *operands)


def body(queries, key_cache, value_cache, draft_keys, draft_values, ancestors, context_length):
    n = lax.axis_size("ctx")
    d = lax.axis_index("ctx")
    layers, rows, q_cols = queries.shape
    assert n == KVH * layers
    kv_cols = draft_keys.shape[2]
    local_len = key_cache.shape[1]
    trees = ancestors.shape[0]
    heads_here = H // n
    score_scale = 1.0 / math.sqrt(DH)
    own = d % layers
    swap = [(s, s ^ 1) for s in range(n)]

    other = 1 - own
    swapped = [
        lax.ppermute(lax.dynamic_index_in_dim(a, other, 0, keepdims=False), "ctx", swap)
        for a in (queries, draft_keys, draft_values)
    ]
    mine_now = [lax.dynamic_index_in_dim(a, own, 0, keepdims=False) for a in (queries, draft_keys, draft_values)]
    first = [jnp.where(own == 0, a, b) for a, b in zip(mine_now, swapped)]
    second = [jnp.where(own == 0, b, a) for a, b in zip(mine_now, swapped)]

    keys_out = jnp.transpose(key_cache.reshape(layers, local_len, KVH, DH), (2, 0, 1, 3))
    values_out = jnp.transpose(value_cache.reshape(layers, local_len, KVH, DH), (2, 0, 1, 3))
    kv = jnp.stack([keys_out, values_out], 2).reshape(n, 2, local_len, DH)
    blocks = lax.all_to_all(kv, "ctx", 0, 0, tiled=True)

    tree_keep = (
        jnp.eye(trees, dtype=jnp.int32)[:, None, :, None] * ancestors[:, :, None, :]
    ).reshape(rows, rows)
    own_q = jnp.transpose(mine_now[0].reshape(rows, heads_here, DH), (1, 0, 2))
    other_q = jnp.transpose(swapped[0].reshape(rows, heads_here, DH), (1, 0, 2))
    draft_k = jnp.concatenate([first[1], second[1]], 1)
    draft_vt = jnp.concatenate([first[2], second[2]], 1)
    tree_cols = jnp.tile(jnp.transpose(tree_keep), (1, heads_here))
    give = attend(context_length, other_q.reshape(heads_here * rows, DH), blocks, draft_k, draft_vt, tree_cols,
                  heads_here)
    got = lax.ppermute(give, "ctx", swap)
    keep = attend(context_length, own_q.reshape(heads_here * rows, DH), blocks, draft_k, draft_vt, tree_cols,
                  heads_here)
    keep = keep[None]
    got = got[None]
    result = jnp.zeros((layers, rows, heads_here * DH), jnp.float32)
    result = lax.dynamic_update_slice(result, keep, (own, 0, 0))
    return lax.dynamic_update_slice(result, got, (other, 0, 0))


def solution(mesh):
    placed = (
        P("req", None, "ctx"),
        P("req", "ctx", None),
        P("req", "ctx", None),
        P("req", None, "ctx"),
        P("req", None, "ctx"),
        P("req", None, None),
        P("req"),
    )
    return jax.shard_map(
        body, mesh=mesh, in_specs=placed, out_specs=P("req", None, "ctx"), check_vma=False
    )
```

```python
import math

import jax
import jax.numpy as jnp
from jax import lax
from jax.experimental import pallas as pl
from jax.experimental.pallas import tpu as pltpu
from jax.sharding import PartitionSpec as P

H = 64
KVH = 8
DH = 128


masked_score = -1e30


def send_target(s, j, n):
    return (s + j) % n if (s + j) % 2 == 0 else (s - j) % n


def blocks_partial(query_heads, block_keys, block_values, draft_k, draft_v, cache_keep, draft_keep, score_scale):
    scores = (
        jnp.einsum("qhd,jpd->hqjp", query_heads, block_keys, preferred_element_type=jnp.float32)
        * score_scale
    )
    draft_scores = (
        jnp.einsum("qhd,td->hqt", query_heads, draft_k, preferred_element_type=jnp.float32)
        * score_scale
    )
    scores = jnp.where(cache_keep[None, None], scores, masked_score)
    draft_scores = jnp.where(draft_keep[None], draft_scores[:, :, None, :], masked_score)
    top_score = jnp.maximum(jnp.max(scores, -1), jnp.max(draft_scores, -1))
    shift_by = jnp.where(top_score > -1e29, top_score, 0.0)
    cache_weight = jnp.exp(scores - shift_by[..., None])
    draft_weight = jnp.exp(draft_scores - shift_by[..., None])
    total = jnp.sum(cache_weight, -1) + jnp.sum(draft_weight, -1)
    weighted = jnp.einsum(
        "hqjp,jpd->hqjd",
        cache_weight.astype(jnp.bfloat16),
        block_values,
        preferred_element_type=jnp.float32,
    )
    weighted = weighted + jnp.einsum(
        "hqjt,td->hqjd",
        draft_weight.astype(jnp.bfloat16),
        draft_v,
        preferred_element_type=jnp.float32,
    )
    alive = total > 0.0
    safe_total = jnp.where(alive, total, 1.0)
    output = lax.reduce_precision(
        jnp.where(alive[..., None], weighted / safe_total[..., None], 0.0), exponent_bits=8, mantissa_bits=7
    )
    lse = jnp.where(alive, top_score + jnp.log(safe_total), masked_score)
    top = jnp.max(lse, -1)
    factor = jnp.where(lse > -1e29, jnp.exp(lse - top[..., None]), 0.0)
    return top, jnp.sum(factor, -1), jnp.sum(factor[..., None] * output, 2)


def _dot(a, b, dims):
    return lax.dot_general(a, b, dims, preferred_element_type=jnp.float32)


def attend_kernel(len_ref, q_ref, kv_ref, dk_ref, dvt_ref, tree_ref, o_ref, out_sc, lse_sc):
    blocks, _, block_len, _ = kv_ref.shape
    score_scale = 1.0 / math.sqrt(DH)
    nt = (((1,), (1,)), ((), ()))
    tn = (((0,), (0,)), ((), ()))
    q = q_ref[...]
    ctx_len = len_ref[0]
    all_keys = kv_ref[:, 0].reshape(blocks * block_len, DH)
    all_scores = _dot(all_keys, q, nt) * score_scale
    pos = lax.broadcasted_iota(jnp.int32, all_scores.shape, 0)
    all_scores = jnp.where(pos < ctx_len, all_scores, masked_score)
    for j in range(blocks):
        scores = all_scores[j * block_len:(j + 1) * block_len]
        top = jnp.max(scores, axis=0, keepdims=True)
        if j == 0:
            draft = _dot(dk_ref[...], q, nt) * score_scale
            draft = jnp.where(tree_ref[...] > 0, draft, masked_score)
            top = jnp.maximum(top, jnp.max(draft, axis=0, keepdims=True))
        shift = jnp.where(top > -1e29, top, 0.0)
        weight = jnp.exp(scores - shift)
        total = jnp.sum(weight, axis=0, keepdims=True)
        acc = _dot(kv_ref[j, 1], weight.astype(jnp.bfloat16), tn)
        if j == 0:
            draft_weight = jnp.exp(draft - shift)
            total = total + jnp.sum(draft_weight, axis=0, keepdims=True)
            acc = acc + _dot(dvt_ref[...], draft_weight.astype(jnp.bfloat16), tn)
        alive = total > 0.0
        safe = jnp.where(alive, total, 1.0)
        out_sc[j] = jnp.where(alive, acc / safe, 0.0).astype(jnp.bfloat16).astype(jnp.float32)
        lse_sc[j:j + 1, :] = jnp.where(alive, top + jnp.log(safe), masked_score)
    lse = lse_sc[...]
    overall = jnp.max(lse, axis=0, keepdims=True)
    factor = jnp.exp(lse - overall)
    weighted = factor[0:1] * out_sc[0]
    for j in range(1, blocks):
        weighted = weighted + factor[j:j + 1] * out_sc[j]
    final = jnp.transpose(weighted / jnp.sum(factor, axis=0, keepdims=True))
    rows = o_ref.shape[0]
    for i in range(o_ref.shape[1] // DH):
        o_ref[:, i * DH:(i + 1) * DH] = final[i * rows:(i + 1) * rows, :]


def attend(context_length, q_rows, blocks_kv, draft_k, draft_vt, tree_cols, heads):
    rows = q_rows.shape[0]
    blocks = blocks_kv.shape[0]
    vmem = pl.BlockSpec(memory_space=pltpu.VMEM)
    operands = [pltpu.with_memory_space_constraint(a, pltpu.VMEM)
                for a in (q_rows, blocks_kv, draft_k, draft_vt, tree_cols)]
    return pl.pallas_call(
        attend_kernel,
        out_shape=jax.ShapeDtypeStruct((rows // heads, heads * DH), jnp.float32),
        in_specs=[pl.BlockSpec(memory_space=pltpu.SMEM)] + [vmem] * 5,
        out_specs=vmem,
        scratch_shapes=[pltpu.VMEM((blocks, DH, rows), jnp.float32), pltpu.VMEM((blocks, rows), jnp.float32)],
    )(context_length, *operands)


def pack_kernel(k_ref, v_ref, o_ref, sem):
    layers, _, width = k_ref.shape
    copies = []
    for k in range(width // DH):
        for l in range(layers):
            for c, src in enumerate((k_ref, v_ref)):
                copy = pltpu.make_async_copy(
                    src.at[l, :, pl.ds(k * DH, DH)], o_ref.at[k * layers + l, c], sem.at[len(copies)]
                )
                copy.start()
                copies.append(copy)
    for copy in copies:
        copy.wait()


def pack(key_cache, value_cache):
    layers, local_len, width = key_cache.shape
    n = layers * (width // DH)
    anywhere = pl.BlockSpec(memory_space=pl.ANY)
    return pl.pallas_call(
        pack_kernel,
        out_shape=jax.ShapeDtypeStruct((n, 2, local_len, DH), key_cache.dtype),
        in_specs=[anywhere, anywhere],
        out_specs=anywhere,
        scratch_shapes=[pltpu.SemaphoreType.DMA((2 * n,))],
    )(key_cache, value_cache)


def body(queries, key_cache, value_cache, draft_keys, draft_values, ancestors, context_length):
    n = lax.axis_size("ctx")
    d = lax.axis_index("ctx")
    layers, rows, q_cols = queries.shape
    assert n == KVH * layers
    kv_cols = draft_keys.shape[2]
    local_len = key_cache.shape[1]
    trees = ancestors.shape[0]
    heads_here = H // n
    score_scale = 1.0 / math.sqrt(DH)
    own = d % layers
    swap = [(s, s ^ 1) for s in range(n)]

    other = 1 - own
    swapped = [
        lax.ppermute(lax.dynamic_index_in_dim(a, other, 0, keepdims=False), "ctx", swap)
        for a in (queries, draft_keys, draft_values)
    ]
    mine_now = [lax.dynamic_index_in_dim(a, own, 0, keepdims=False) for a in (queries, draft_keys, draft_values)]
    first = [jnp.where(own == 0, a, b) for a, b in zip(mine_now, swapped)]
    second = [jnp.where(own == 0, b, a) for a, b in zip(mine_now, swapped)]

    kv = pack(key_cache, value_cache)
    blocks = lax.all_to_all(kv, "ctx", 0, 0, tiled=True)

    tree_keep = (
        jnp.eye(trees, dtype=jnp.int32)[:, None, :, None] * ancestors[:, :, None, :]
    ).reshape(rows, rows)
    own_q = jnp.transpose(mine_now[0].reshape(rows, heads_here, DH), (1, 0, 2))
    other_q = jnp.transpose(swapped[0].reshape(rows, heads_here, DH), (1, 0, 2))
    draft_k = jnp.concatenate([first[1], second[1]], 1)
    draft_vt = jnp.concatenate([first[2], second[2]], 1)
    tree_cols = jnp.tile(jnp.transpose(tree_keep), (1, heads_here))
    give = attend(context_length, other_q.reshape(heads_here * rows, DH), blocks, draft_k, draft_vt, tree_cols,
                  heads_here)
    got = lax.ppermute(give, "ctx", swap)
    keep = attend(context_length, own_q.reshape(heads_here * rows, DH), blocks, draft_k, draft_vt, tree_cols,
                  heads_here)
    keep = keep[None]
    got = got[None]
    result = jnp.zeros((layers, rows, heads_here * DH), jnp.float32)
    result = lax.dynamic_update_slice(result, keep, (own, 0, 0))
    return lax.dynamic_update_slice(result, got, (other, 0, 0))


def solution(mesh):
    placed = (
        P("req", None, "ctx"),
        P("req", "ctx", None),
        P("req", "ctx", None),
        P("req", None, "ctx"),
        P("req", None, "ctx"),
        P("req", None, None),
        P("req"),
    )
    return jax.shard_map(
        body, mesh=mesh, in_specs=placed, out_specs=P("req", None, "ctx"), check_vma=False
    )
```

```python
import math

import jax
import jax.numpy as jnp
from jax import lax
from jax.experimental import pallas as pl
from jax.experimental.pallas import tpu as pltpu
from jax.sharding import PartitionSpec as P

H = 64
KVH = 8
DH = 128


masked_score = -1e30


def send_target(s, j, n):
    return (s + j) % n if (s + j) % 2 == 0 else (s - j) % n


def blocks_partial(query_heads, block_keys, block_values, draft_k, draft_v, cache_keep, draft_keep, score_scale):
    scores = (
        jnp.einsum("qhd,jpd->hqjp", query_heads, block_keys, preferred_element_type=jnp.float32)
        * score_scale
    )
    draft_scores = (
        jnp.einsum("qhd,td->hqt", query_heads, draft_k, preferred_element_type=jnp.float32)
        * score_scale
    )
    scores = jnp.where(cache_keep[None, None], scores, masked_score)
    draft_scores = jnp.where(draft_keep[None], draft_scores[:, :, None, :], masked_score)
    top_score = jnp.maximum(jnp.max(scores, -1), jnp.max(draft_scores, -1))
    shift_by = jnp.where(top_score > -1e29, top_score, 0.0)
    cache_weight = jnp.exp(scores - shift_by[..., None])
    draft_weight = jnp.exp(draft_scores - shift_by[..., None])
    total = jnp.sum(cache_weight, -1) + jnp.sum(draft_weight, -1)
    weighted = jnp.einsum(
        "hqjp,jpd->hqjd",
        cache_weight.astype(jnp.bfloat16),
        block_values,
        preferred_element_type=jnp.float32,
    )
    weighted = weighted + jnp.einsum(
        "hqjt,td->hqjd",
        draft_weight.astype(jnp.bfloat16),
        draft_v,
        preferred_element_type=jnp.float32,
    )
    alive = total > 0.0
    safe_total = jnp.where(alive, total, 1.0)
    output = lax.reduce_precision(
        jnp.where(alive[..., None], weighted / safe_total[..., None], 0.0), exponent_bits=8, mantissa_bits=7
    )
    lse = jnp.where(alive, top_score + jnp.log(safe_total), masked_score)
    top = jnp.max(lse, -1)
    factor = jnp.where(lse > -1e29, jnp.exp(lse - top[..., None]), 0.0)
    return top, jnp.sum(factor, -1), jnp.sum(factor[..., None] * output, 2)


def _dot(a, b, dims):
    return lax.dot_general(a, b, dims, preferred_element_type=jnp.float32)


def attend_kernel(len_ref, q_ref, kv_ref, dk_ref, dvt_ref, tree_ref, o_ref, out_sc, lse_sc):
    blocks, _, block_len, _ = kv_ref.shape
    score_scale = 1.0 / math.sqrt(DH)
    nt = (((1,), (1,)), ((), ()))
    tn = (((0,), (0,)), ((), ()))
    q = q_ref[...]
    ctx_len = len_ref[0]
    all_keys = kv_ref[:, 0].reshape(blocks * block_len, DH)
    all_scores = _dot(all_keys, q, nt) * score_scale
    pos = lax.broadcasted_iota(jnp.int32, all_scores.shape, 0)
    all_scores = jnp.where(pos < ctx_len, all_scores, masked_score)
    for j in range(blocks):
        scores = all_scores[j * block_len:(j + 1) * block_len]
        top = jnp.max(scores, axis=0, keepdims=True)
        if j == 0:
            draft = _dot(dk_ref[...], q, nt) * score_scale
            draft = jnp.where(tree_ref[...] > 0, draft, masked_score)
            top = jnp.maximum(top, jnp.max(draft, axis=0, keepdims=True))
        shift = jnp.where(top > -1e29, top, 0.0)
        weight = jnp.exp(scores - shift)
        total = jnp.sum(weight, axis=0, keepdims=True)
        acc = _dot(kv_ref[j, 1], weight.astype(jnp.bfloat16), tn)
        if j == 0:
            draft_weight = jnp.exp(draft - shift)
            total = total + jnp.sum(draft_weight, axis=0, keepdims=True)
            acc = acc + _dot(dvt_ref[...], draft_weight.astype(jnp.bfloat16), tn)
        alive = total > 0.0
        safe = jnp.where(alive, total, 1.0)
        out_sc[j] = jnp.where(alive, acc / safe, 0.0).astype(jnp.bfloat16).astype(jnp.float32)
        lse_sc[j:j + 1, :] = jnp.where(alive, top + jnp.log(safe), masked_score)
    lse = lse_sc[...]
    overall = jnp.max(lse, axis=0, keepdims=True)
    factor = jnp.exp(lse - overall)
    weighted = factor[0:1] * out_sc[0]
    for j in range(1, blocks):
        weighted = weighted + factor[j:j + 1] * out_sc[j]
    final = jnp.transpose(weighted / jnp.sum(factor, axis=0, keepdims=True))
    rows = o_ref.shape[0]
    for i in range(o_ref.shape[1] // DH):
        o_ref[:, i * DH:(i + 1) * DH] = final[i * rows:(i + 1) * rows, :]


def attend(context_length, q_rows, blocks_kv, draft_k, draft_vt, tree_cols, heads):
    rows = q_rows.shape[0]
    blocks = blocks_kv.shape[0]
    vmem = pl.BlockSpec(memory_space=pltpu.VMEM)
    operands = [pltpu.with_memory_space_constraint(a, pltpu.VMEM)
                for a in (q_rows, blocks_kv, draft_k, draft_vt, tree_cols)]
    return pl.pallas_call(
        attend_kernel,
        out_shape=jax.ShapeDtypeStruct((rows // heads, heads * DH), jnp.float32),
        in_specs=[pl.BlockSpec(memory_space=pltpu.SMEM)] + [vmem] * 5,
        out_specs=vmem,
        scratch_shapes=[pltpu.VMEM((blocks, DH, rows), jnp.float32), pltpu.VMEM((blocks, rows), jnp.float32)],
    )(context_length, *operands)


def pack_kernel(k_ref, v_ref, o_ref):
    layers, _, width = k_ref.shape
    for k in range(width // DH):
        for l in range(layers):
            o_ref[k * layers + l, 0] = k_ref[l, :, k * DH:(k + 1) * DH]
            o_ref[k * layers + l, 1] = v_ref[l, :, k * DH:(k + 1) * DH]


def pack(key_cache, value_cache):
    layers, local_len, width = key_cache.shape
    n = layers * (width // DH)
    vmem = pl.BlockSpec(memory_space=pltpu.VMEM)
    return pl.pallas_call(
        pack_kernel,
        out_shape=jax.ShapeDtypeStruct((n, 2, local_len, DH), key_cache.dtype),
        in_specs=[vmem, vmem],
        out_specs=vmem,
    )(key_cache, value_cache)


def body(queries, key_cache, value_cache, draft_keys, draft_values, ancestors, context_length):
    n = lax.axis_size("ctx")
    d = lax.axis_index("ctx")
    layers, rows, q_cols = queries.shape
    assert n == KVH * layers
    kv_cols = draft_keys.shape[2]
    local_len = key_cache.shape[1]
    trees = ancestors.shape[0]
    heads_here = H // n
    score_scale = 1.0 / math.sqrt(DH)
    own = d % layers
    swap = [(s, s ^ 1) for s in range(n)]

    other = 1 - own
    swapped = [
        lax.ppermute(lax.dynamic_index_in_dim(a, other, 0, keepdims=False), "ctx", swap)
        for a in (queries, draft_keys, draft_values)
    ]
    mine_now = [lax.dynamic_index_in_dim(a, own, 0, keepdims=False) for a in (queries, draft_keys, draft_values)]
    first = [jnp.where(own == 0, a, b) for a, b in zip(mine_now, swapped)]
    second = [jnp.where(own == 0, b, a) for a, b in zip(mine_now, swapped)]

    kv = pack(key_cache, value_cache)
    blocks = lax.all_to_all(kv, "ctx", 0, 0, tiled=True)

    tree_keep = (
        jnp.eye(trees, dtype=jnp.int32)[:, None, :, None] * ancestors[:, :, None, :]
    ).reshape(rows, rows)
    own_q = jnp.transpose(mine_now[0].reshape(rows, heads_here, DH), (1, 0, 2))
    other_q = jnp.transpose(swapped[0].reshape(rows, heads_here, DH), (1, 0, 2))
    draft_k = jnp.concatenate([first[1], second[1]], 1)
    draft_vt = jnp.concatenate([first[2], second[2]], 1)
    tree_cols = jnp.tile(jnp.transpose(tree_keep), (1, heads_here))
    give = attend(context_length, other_q.reshape(heads_here * rows, DH), blocks, draft_k, draft_vt, tree_cols,
                  heads_here)
    got = lax.ppermute(give, "ctx", swap)
    keep = attend(context_length, own_q.reshape(heads_here * rows, DH), blocks, draft_k, draft_vt, tree_cols,
                  heads_here)
    keep = keep[None]
    got = got[None]
    result = jnp.zeros((layers, rows, heads_here * DH), jnp.float32)
    result = lax.dynamic_update_slice(result, keep, (own, 0, 0))
    return lax.dynamic_update_slice(result, got, (other, 0, 0))


def solution(mesh):
    placed = (
        P("req", None, "ctx"),
        P("req", "ctx", None),
        P("req", "ctx", None),
        P("req", None, "ctx"),
        P("req", None, "ctx"),
        P("req", None, None),
        P("req"),
    )
    return jax.shard_map(
        body, mesh=mesh, in_specs=placed, out_specs=P("req", None, "ctx"), check_vma=False
    )
```

```python
import math

import jax
import jax.numpy as jnp
from jax import lax
from jax.experimental import pallas as pl
from jax.experimental.pallas import tpu as pltpu
from jax.sharding import PartitionSpec as P

H = 64
KVH = 8
DH = 128


masked_score = -1e30


def send_target(s, j, n):
    return (s + j) % n if (s + j) % 2 == 0 else (s - j) % n


def blocks_partial(query_heads, block_keys, block_values, draft_k, draft_v, cache_keep, draft_keep, score_scale):
    scores = (
        jnp.einsum("qhd,jpd->hqjp", query_heads, block_keys, preferred_element_type=jnp.float32)
        * score_scale
    )
    draft_scores = (
        jnp.einsum("qhd,td->hqt", query_heads, draft_k, preferred_element_type=jnp.float32)
        * score_scale
    )
    scores = jnp.where(cache_keep[None, None], scores, masked_score)
    draft_scores = jnp.where(draft_keep[None], draft_scores[:, :, None, :], masked_score)
    top_score = jnp.maximum(jnp.max(scores, -1), jnp.max(draft_scores, -1))
    shift_by = jnp.where(top_score > -1e29, top_score, 0.0)
    cache_weight = jnp.exp(scores - shift_by[..., None])
    draft_weight = jnp.exp(draft_scores - shift_by[..., None])
    total = jnp.sum(cache_weight, -1) + jnp.sum(draft_weight, -1)
    weighted = jnp.einsum(
        "hqjp,jpd->hqjd",
        cache_weight.astype(jnp.bfloat16),
        block_values,
        preferred_element_type=jnp.float32,
    )
    weighted = weighted + jnp.einsum(
        "hqjt,td->hqjd",
        draft_weight.astype(jnp.bfloat16),
        draft_v,
        preferred_element_type=jnp.float32,
    )
    alive = total > 0.0
    safe_total = jnp.where(alive, total, 1.0)
    output = lax.reduce_precision(
        jnp.where(alive[..., None], weighted / safe_total[..., None], 0.0), exponent_bits=8, mantissa_bits=7
    )
    lse = jnp.where(alive, top_score + jnp.log(safe_total), masked_score)
    top = jnp.max(lse, -1)
    factor = jnp.where(lse > -1e29, jnp.exp(lse - top[..., None]), 0.0)
    return top, jnp.sum(factor, -1), jnp.sum(factor[..., None] * output, 2)


def _dot(a, b, dims):
    return lax.dot_general(a, b, dims, preferred_element_type=jnp.float32)


def attend_kernel(len_ref, q_ref, kv_ref, dk_ref, dvt_ref, tree_ref, give_ref, keep_ref, out_sc, lse_sc):
    blocks, _, block_len, _ = kv_ref.shape
    score_scale = 1.0 / math.sqrt(DH)
    nt = (((1,), (1,)), ((), ()))
    tn = (((0,), (0,)), ((), ()))
    q = q_ref[...]
    ctx_len = len_ref[0]
    all_keys = kv_ref[:, 0].reshape(blocks * block_len, DH)
    all_scores = _dot(all_keys, q, nt) * score_scale
    pos = lax.broadcasted_iota(jnp.int32, all_scores.shape, 0)
    all_scores = jnp.where(pos < ctx_len, all_scores, masked_score)
    for j in range(blocks):
        scores = all_scores[j * block_len:(j + 1) * block_len]
        top = jnp.max(scores, axis=0, keepdims=True)
        if j == 0:
            draft = _dot(dk_ref[...], q, nt) * score_scale
            draft = jnp.where(tree_ref[...] > 0, draft, masked_score)
            top = jnp.maximum(top, jnp.max(draft, axis=0, keepdims=True))
        shift = jnp.where(top > -1e29, top, 0.0)
        weight = jnp.exp(scores - shift)
        total = jnp.sum(weight, axis=0, keepdims=True)
        acc = _dot(kv_ref[j, 1], weight.astype(jnp.bfloat16), tn)
        if j == 0:
            draft_weight = jnp.exp(draft - shift)
            total = total + jnp.sum(draft_weight, axis=0, keepdims=True)
            acc = acc + _dot(dvt_ref[...], draft_weight.astype(jnp.bfloat16), tn)
        alive = total > 0.0
        safe = jnp.where(alive, total, 1.0)
        out_sc[j] = jnp.where(alive, acc / safe, 0.0).astype(jnp.bfloat16).astype(jnp.float32)
        lse_sc[j:j + 1, :] = jnp.where(alive, top + jnp.log(safe), masked_score)
    lse = lse_sc[...]
    overall = jnp.max(lse, axis=0, keepdims=True)
    factor = jnp.exp(lse - overall)
    weighted = factor[0:1] * out_sc[0]
    for j in range(1, blocks):
        weighted = weighted + factor[j:j + 1] * out_sc[j]
    final = jnp.transpose(weighted / jnp.sum(factor, axis=0, keepdims=True))
    rows = give_ref.shape[0]
    heads = give_ref.shape[1] // DH
    for h, o_ref in enumerate((give_ref, keep_ref)):
        for i in range(heads):
            o_ref[:, i * DH:(i + 1) * DH] = final[(h * heads + i) * rows:(h * heads + i + 1) * rows, :]


def attend(context_length, q_rows, blocks_kv, draft_k, draft_vt, tree_cols, heads):
    rows = q_rows.shape[0]
    blocks = blocks_kv.shape[0]
    vmem = pl.BlockSpec(memory_space=pltpu.VMEM)
    operands = [pltpu.with_memory_space_constraint(a, pltpu.VMEM)
                for a in (q_rows, blocks_kv, draft_k, draft_vt, tree_cols)]
    return pl.pallas_call(
        attend_kernel,
        out_shape=[jax.ShapeDtypeStruct((rows // heads, heads * DH // 2), jnp.float32)] * 2,
        in_specs=[pl.BlockSpec(memory_space=pltpu.SMEM)] + [vmem] * 5,
        out_specs=[vmem, vmem],
        scratch_shapes=[pltpu.VMEM((blocks, DH, rows), jnp.float32), pltpu.VMEM((blocks, rows), jnp.float32)],
    )(context_length, *operands)


def body(queries, key_cache, value_cache, draft_keys, draft_values, ancestors, context_length):
    n = lax.axis_size("ctx")
    d = lax.axis_index("ctx")
    layers, rows, q_cols = queries.shape
    assert n == KVH * layers
    kv_cols = draft_keys.shape[2]
    local_len = key_cache.shape[1]
    trees = ancestors.shape[0]
    heads_here = H // n
    score_scale = 1.0 / math.sqrt(DH)
    own = d % layers
    swap = [(s, s ^ 1) for s in range(n)]

    other = 1 - own
    swapped = [
        lax.ppermute(lax.dynamic_index_in_dim(a, other, 0, keepdims=False), "ctx", swap)
        for a in (queries, draft_keys, draft_values)
    ]
    mine_now = [lax.dynamic_index_in_dim(a, own, 0, keepdims=False) for a in (queries, draft_keys, draft_values)]
    first = [jnp.where(own == 0, a, b) for a, b in zip(mine_now, swapped)]
    second = [jnp.where(own == 0, b, a) for a, b in zip(mine_now, swapped)]

    keys_out = jnp.transpose(key_cache.reshape(layers, local_len, KVH, DH), (2, 0, 1, 3))
    values_out = jnp.transpose(value_cache.reshape(layers, local_len, KVH, DH), (2, 0, 1, 3))
    kv = jnp.stack([keys_out, values_out], 2).reshape(n, 2, local_len, DH)
    blocks = lax.all_to_all(kv, "ctx", 0, 0, tiled=True)

    tree_keep = (
        jnp.eye(trees, dtype=jnp.int32)[:, None, :, None] * ancestors[:, :, None, :]
    ).reshape(rows, rows)
    own_q = jnp.transpose(mine_now[0].reshape(rows, heads_here, DH), (1, 0, 2))
    other_q = jnp.transpose(swapped[0].reshape(rows, heads_here, DH), (1, 0, 2))
    draft_k = jnp.concatenate([first[1], second[1]], 1)
    draft_vt = jnp.concatenate([first[2], second[2]], 1)
    tree_cols = jnp.tile(jnp.transpose(tree_keep), (1, heads_here))
    both_q = jnp.concatenate([other_q, own_q], 0).reshape(2 * heads_here * rows, DH)
    give, keep = attend(context_length, both_q, blocks, draft_k, draft_vt, jnp.tile(tree_cols, (1, 2)), 2 * heads_here)
    got = lax.ppermute(give, "ctx", swap)
    keep = keep[None]
    got = got[None]
    result = jnp.zeros((layers, rows, heads_here * DH), jnp.float32)
    result = lax.dynamic_update_slice(result, keep, (own, 0, 0))
    return lax.dynamic_update_slice(result, got, (other, 0, 0))


def solution(mesh):
    placed = (
        P("req", None, "ctx"),
        P("req", "ctx", None),
        P("req", "ctx", None),
        P("req", None, "ctx"),
        P("req", None, "ctx"),
        P("req", None, None),
        P("req"),
    )
    return jax.shard_map(
        body, mesh=mesh, in_specs=placed, out_specs=P("req", None, "ctx"), check_vma=False
    )
```

```python
import math

import jax
import jax.numpy as jnp
from jax import lax
from jax.experimental import pallas as pl
from jax.experimental.pallas import tpu as pltpu
from jax.sharding import PartitionSpec as P

H = 64
KVH = 8
DH = 128


masked_score = -1e30


def _dot(a, b, dims):
    return lax.dot_general(a, b, dims, preferred_element_type=jnp.float32)


def attend_kernel(len_ref, q_ref, kv_ref, dk_ref, dvt_ref, tree_ref, give_ref, keep_ref, out_sc, lse_sc):
    blocks, _, block_len, _ = kv_ref.shape
    score_scale = 1.0 / math.sqrt(DH)
    nt = (((1,), (1,)), ((), ()))
    tn = (((0,), (0,)), ((), ()))
    q = q_ref[...]
    ctx_len = len_ref[0]
    all_keys = kv_ref[:, 0].reshape(blocks * block_len, DH)
    all_scores = _dot(all_keys, q, nt) * score_scale
    pos = lax.broadcasted_iota(jnp.int32, all_scores.shape, 0)
    all_scores = jnp.where(pos < ctx_len, all_scores, masked_score)
    for j in range(blocks):
        scores = all_scores[j * block_len:(j + 1) * block_len]
        top = jnp.max(scores, axis=0, keepdims=True)
        if j == 0:
            draft = _dot(dk_ref[...], q, nt) * score_scale
            draft = jnp.where(tree_ref[...] > 0, draft, masked_score)
            top = jnp.maximum(top, jnp.max(draft, axis=0, keepdims=True))
        shift = jnp.where(top > -1e29, top, 0.0)
        weight = jnp.exp(scores - shift)
        total = jnp.sum(weight, axis=0, keepdims=True)
        acc = _dot(kv_ref[j, 1], weight.astype(jnp.bfloat16), tn)
        if j == 0:
            draft_weight = jnp.exp(draft - shift)
            total = total + jnp.sum(draft_weight, axis=0, keepdims=True)
            acc = acc + _dot(dvt_ref[...], draft_weight.astype(jnp.bfloat16), tn)
        alive = total > 0.0
        safe = jnp.where(alive, total, 1.0)
        out_sc[j] = jnp.where(alive, acc / safe, 0.0).astype(jnp.bfloat16).astype(jnp.float32)
        lse_sc[j:j + 1, :] = jnp.where(alive, top + jnp.log(safe), masked_score)
    lse = lse_sc[...]
    overall = jnp.max(lse, axis=0, keepdims=True)
    factor = jnp.exp(lse - overall)
    weighted = factor[0:1] * out_sc[0]
    for j in range(1, blocks):
        weighted = weighted + factor[j:j + 1] * out_sc[j]
    final = jnp.transpose(weighted / jnp.sum(factor, axis=0, keepdims=True))
    rows = give_ref.shape[0]
    heads = give_ref.shape[1] // DH
    for h, o_ref in enumerate((give_ref, keep_ref)):
        for i in range(heads):
            o_ref[:, i * DH:(i + 1) * DH] = final[(h * heads + i) * rows:(h * heads + i + 1) * rows, :]


def attend(context_length, q_rows, blocks_kv, draft_k, draft_vt, tree_cols, heads):
    rows = q_rows.shape[0]
    blocks = blocks_kv.shape[0]
    vmem = pl.BlockSpec(memory_space=pltpu.VMEM)
    operands = [pltpu.with_memory_space_constraint(a, pltpu.VMEM)
                for a in (q_rows, blocks_kv, draft_k, draft_vt, tree_cols)]
    return pl.pallas_call(
        attend_kernel,
        out_shape=[jax.ShapeDtypeStruct((rows // heads, heads * DH // 2), jnp.float32)] * 2,
        in_specs=[pl.BlockSpec(memory_space=pltpu.SMEM)] + [vmem] * 5,
        out_specs=[vmem, vmem],
        scratch_shapes=[pltpu.VMEM((blocks, DH, rows), jnp.float32), pltpu.VMEM((blocks, rows), jnp.float32)],
    )(context_length, *operands)


def body(queries, key_cache, value_cache, draft_keys, draft_values, ancestors, context_length):
    n = lax.axis_size("ctx")
    d = lax.axis_index("ctx")
    layers, rows, q_cols = queries.shape
    assert n == KVH * layers
    local_len = key_cache.shape[1]
    trees = ancestors.shape[0]
    heads_here = H // n
    own = d % layers
    swap = [(s, s ^ 1) for s in range(n)]

    other = 1 - own
    swapped = [
        lax.ppermute(lax.dynamic_index_in_dim(a, other, 0, keepdims=False), "ctx", swap)
        for a in (queries, draft_keys, draft_values)
    ]
    mine_now = [lax.dynamic_index_in_dim(a, own, 0, keepdims=False) for a in (queries, draft_keys, draft_values)]
    first = [jnp.where(own == 0, a, b) for a, b in zip(mine_now, swapped)]
    second = [jnp.where(own == 0, b, a) for a, b in zip(mine_now, swapped)]

    keys_out = jnp.transpose(key_cache.reshape(layers, local_len, KVH, DH), (2, 0, 1, 3))
    values_out = jnp.transpose(value_cache.reshape(layers, local_len, KVH, DH), (2, 0, 1, 3))
    kv = jnp.stack([keys_out, values_out], 2).reshape(n, 2, local_len, DH)
    blocks = lax.all_to_all(kv, "ctx", 0, 0, tiled=True)

    tree_keep = (
        jnp.eye(trees, dtype=jnp.int32)[:, None, :, None] * ancestors[:, :, None, :]
    ).reshape(rows, rows)
    own_q = jnp.transpose(mine_now[0].reshape(rows, heads_here, DH), (1, 0, 2))
    other_q = jnp.transpose(swapped[0].reshape(rows, heads_here, DH), (1, 0, 2))
    draft_k = jnp.concatenate([first[1], second[1]], 1)
    draft_vt = jnp.concatenate([first[2], second[2]], 1)
    tree_cols = jnp.tile(jnp.transpose(tree_keep), (1, heads_here))
    both_q = jnp.concatenate([other_q, own_q], 0).reshape(2 * heads_here * rows, DH)
    give, keep = attend(context_length, both_q, blocks, draft_k, draft_vt, jnp.tile(tree_cols, (1, 2)), 2 * heads_here)
    got = lax.ppermute(give, "ctx", swap)
    keep = keep[None]
    got = got[None]
    result = jnp.zeros((layers, rows, heads_here * DH), jnp.float32)
    result = lax.dynamic_update_slice(result, keep, (own, 0, 0))
    return lax.dynamic_update_slice(result, got, (other, 0, 0))


def solution(mesh):
    placed = (
        P("req", None, "ctx"),
        P("req", "ctx", None),
        P("req", "ctx", None),
        P("req", None, "ctx"),
        P("req", None, "ctx"),
        P("req", None, None),
        P("req"),
    )
    return jax.shard_map(
        body, mesh=mesh, in_specs=placed, out_specs=P("req", None, "ctx"), check_vma=False
    )
```

```python
import math

import jax
import jax.numpy as jnp
from jax import lax
from jax.experimental import pallas as pl
from jax.experimental.pallas import tpu as pltpu
from jax.sharding import PartitionSpec as P

H = 64
KVH = 8
DH = 128


masked_score = -1e30


def _dot(a, b, dims):
    return lax.dot_general(a, b, dims, preferred_element_type=jnp.float32)


def attend_kernel(len_ref, q_ref, kv_ref, dk_ref, dvt_ref, tree_ref, give_ref, keep_ref, out_sc, lse_sc):
    blocks, _, block_len, _ = kv_ref.shape
    score_scale = 1.0 / math.sqrt(DH)
    nt = (((1,), (1,)), ((), ()))
    tn = (((0,), (0,)), ((), ()))
    q = q_ref[...]
    ctx_len = len_ref[0]
    all_keys = kv_ref[:, 0].reshape(blocks * block_len, DH)
    all_scores = _dot(all_keys, q, nt) * score_scale
    pos = lax.broadcasted_iota(jnp.int32, all_scores.shape, 0)
    all_scores = jnp.where(pos < ctx_len, all_scores, masked_score)
    for j in range(blocks):
        scores = all_scores[j * block_len:(j + 1) * block_len]
        top = jnp.max(scores, axis=0, keepdims=True)
        if j == 0:
            draft = _dot(dk_ref[...], q, nt) * score_scale
            draft = jnp.where(tree_ref[...] > 0, draft, masked_score)
            top = jnp.maximum(top, jnp.max(draft, axis=0, keepdims=True))
        shift = jnp.where(top > -1e29, top, 0.0)
        weight = jnp.exp(scores - shift)
        total = jnp.sum(weight, axis=0, keepdims=True)
        acc = _dot(kv_ref[j, 1], weight.astype(jnp.bfloat16), tn)
        if j == 0:
            draft_weight = jnp.exp(draft - shift)
            total = total + jnp.sum(draft_weight, axis=0, keepdims=True)
            acc = acc + _dot(dvt_ref[...], draft_weight.astype(jnp.bfloat16), tn)
        alive = total > 0.0
        safe = jnp.where(alive, total, 1.0)
        out_sc[j] = jnp.where(alive, acc / safe, 0.0).astype(jnp.bfloat16).astype(jnp.float32)
        lse_sc[j:j + 1, :] = jnp.where(alive, top + jnp.log(safe), masked_score)
    lse = lse_sc[...]
    overall = jnp.max(lse, axis=0, keepdims=True)
    factor = jnp.exp(lse - overall)
    weighted = factor[0:1] * out_sc[0]
    for j in range(1, blocks):
        weighted = weighted + factor[j:j + 1] * out_sc[j]
    final = jnp.transpose(weighted / jnp.sum(factor, axis=0, keepdims=True))
    rows = give_ref.shape[0]
    heads = give_ref.shape[1] // DH
    for h, o_ref in enumerate((give_ref, keep_ref)):
        for i in range(heads):
            o_ref[:, i * DH:(i + 1) * DH] = final[(h * heads + i) * rows:(h * heads + i + 1) * rows, :]


def attend(context_length, q_rows, blocks_kv, draft_k, draft_vt, tree_cols, heads):
    rows = q_rows.shape[0]
    blocks = blocks_kv.shape[0]
    vmem = pl.BlockSpec(memory_space=pltpu.VMEM)
    operands = [pltpu.with_memory_space_constraint(a, pltpu.VMEM)
                for a in (q_rows, blocks_kv, draft_k, draft_vt, tree_cols)]
    return pl.pallas_call(
        attend_kernel,
        out_shape=[jax.ShapeDtypeStruct((rows // heads, heads * DH // 2), jnp.float32)] * 2,
        in_specs=[pl.BlockSpec(memory_space=pltpu.SMEM)] + [vmem] * 5,
        out_specs=[vmem, vmem],
        scratch_shapes=[pltpu.VMEM((blocks, DH, rows), jnp.float32), pltpu.VMEM((blocks, rows), jnp.float32)],
    )(context_length, *operands)


def pack_kernel(k_ref, v_ref, o_ref):
    layers = k_ref.shape[0]
    for h in range(k_ref.shape[2] // DH):
        for l in range(layers):
            o_ref[h * layers + l, 0] = k_ref[l, :, h * DH:(h + 1) * DH]
            o_ref[h * layers + l, 1] = v_ref[l, :, h * DH:(h + 1) * DH]


def pack(key_cache, value_cache, heads_per_step=2):
    layers, local_len, width = key_cache.shape
    steps = width // DH // heads_per_step
    n = layers * (width // DH)
    cache_spec = pl.BlockSpec((layers, local_len, heads_per_step * DH), lambda g: (0, 0, g))
    return pl.pallas_call(
        pack_kernel,
        grid=(steps,),
        out_shape=jax.ShapeDtypeStruct((n, 2, local_len, DH), key_cache.dtype),
        in_specs=[cache_spec, cache_spec],
        out_specs=pl.BlockSpec((heads_per_step * layers, 2, local_len, DH), lambda g: (g, 0, 0, 0)),
    )(key_cache, value_cache)


def body(queries, key_cache, value_cache, draft_keys, draft_values, ancestors, context_length):
    n = lax.axis_size("ctx")
    d = lax.axis_index("ctx")
    layers, rows, q_cols = queries.shape
    assert n == KVH * layers
    local_len = key_cache.shape[1]
    trees = ancestors.shape[0]
    heads_here = H // n
    own = d % layers
    swap = [(s, s ^ 1) for s in range(n)]

    other = 1 - own
    swapped = [
        lax.ppermute(lax.dynamic_index_in_dim(a, other, 0, keepdims=False), "ctx", swap)
        for a in (queries, draft_keys, draft_values)
    ]
    mine_now = [lax.dynamic_index_in_dim(a, own, 0, keepdims=False) for a in (queries, draft_keys, draft_values)]
    first = [jnp.where(own == 0, a, b) for a, b in zip(mine_now, swapped)]
    second = [jnp.where(own == 0, b, a) for a, b in zip(mine_now, swapped)]

    kv = pack(key_cache, value_cache)
    blocks = lax.all_to_all(kv, "ctx", 0, 0, tiled=True)

    tree_keep = (
        jnp.eye(trees, dtype=jnp.int32)[:, None, :, None] * ancestors[:, :, None, :]
    ).reshape(rows, rows)
    own_q = jnp.transpose(mine_now[0].reshape(rows, heads_here, DH), (1, 0, 2))
    other_q = jnp.transpose(swapped[0].reshape(rows, heads_here, DH), (1, 0, 2))
    draft_k = jnp.concatenate([first[1], second[1]], 1)
    draft_vt = jnp.concatenate([first[2], second[2]], 1)
    tree_cols = jnp.tile(jnp.transpose(tree_keep), (1, heads_here))
    both_q = jnp.concatenate([other_q, own_q], 0).reshape(2 * heads_here * rows, DH)
    give, keep = attend(context_length, both_q, blocks, draft_k, draft_vt, jnp.tile(tree_cols, (1, 2)), 2 * heads_here)
    got = lax.ppermute(give, "ctx", swap)
    keep = keep[None]
    got = got[None]
    result = jnp.zeros((layers, rows, heads_here * DH), jnp.float32)
    result = lax.dynamic_update_slice(result, keep, (own, 0, 0))
    return lax.dynamic_update_slice(result, got, (other, 0, 0))


def solution(mesh):
    placed = (
        P("req", None, "ctx"),
        P("req", "ctx", None),
        P("req", "ctx", None),
        P("req", None, "ctx"),
        P("req", None, "ctx"),
        P("req", None, None),
        P("req"),
    )
    return jax.shard_map(
        body, mesh=mesh, in_specs=placed, out_specs=P("req", None, "ctx"), check_vma=False
    )
```
